256 devices in a mesh: lat: 32 (over x, z_lo, core), lev: 8 (over y, z_hi).
Axes of the slice: x: 4, y: 4, z: 8 (z_hi: 2, z_lo: 4; z = z_hi * 4 + z_lo), core: 2. Of those that a mesh axis runs over, the one named last changes fastest.
Arguments:
- zonal_wind: float32 [32, 512, 2880], P('lev', 'lat'), may hold values from -6 to 6
- merid_wind: float32 [32, 512, 2880], P('lev', 'lat'), may hold values from -6 to 6
- tracer: float32 [32, 512, 2880], P('lev', 'lat'), may hold values from -6 to 6
- vertical_wind: float32 [32, 512, 2880], P('lev', 'lat'), may hold values from -6 to 6
- cutoff: int32 [512], replicated, may hold values from 1 to 1440, as said below
Outputs:
- zonal_next: float32 [32, 512, 2880], P('lev', 'lat')
- merid_next: float32 [32, 512, 2880], P('lev', 'lat')
- tracer_next: float32 [32, 512, 2880], P('lev', 'lat')
The draws below stay inside these ranges and needn't reach their ends.
Inputs may be any that keep to these rules, and one draw needn't show every extreme that they name: With d the distance of latitude j in rows from the nearer pole (d = 1 for the first and last latitude): cutoff is 1 at d = 1, 719 at d = 80, between 1 and 719 for d < 80, and 1440 for d > 80.
All inputs are finite; a program needn't handle non-finite values.
Results may differ from the reference program's by a relative error of at most 0.0001.
Values sent between devices are 32-bit elements; how exact they have to be, the bound alone decides.
No kernel may reach another device: no remote copies, remote signals or barrier semaphores. Data moves between devices by JAX's collectives and lax.ppermute only.
A program may use at most 128 MiB of HBM per device.

```python
import math
import jax
import jax.numpy as jnp
from jax import lax

NLON = 2880
KMAX = 720
NLAT = 512
LEVELS = 32
CAP = 80


def draw_cutoff(key, part):
    row_ids = jnp.arange(NLAT, dtype=jnp.int32)
    depths = jnp.minimum(row_ids, NLAT - 1 - row_ids) + 1
    base_step = max(KMAX // CAP, 1)
    slopes = jax.random.randint(key, (NLAT,), max(base_step // 2, 1), 2 * base_step + 1, dtype=jnp.int32)
    rising = jnp.minimum(1 + (depths - 1) * slopes, KMAX - 1)
    rising = jnp.where(depths == CAP, KMAX - 1, rising)
    return jnp.where(depths <= CAP, rising, NLON // 2).astype(jnp.int32)


def block_levels(rng, extent, split, least, largest):
    factor_of, own = 1.0, jax.random.fold_in(rng, 6)
    for position, parts in split:
        draws = jnp.exp(jax.random.uniform(jax.random.fold_in(own, position), (parts,), jnp.float32, least / len(split), largest / len(split)))
        factor_of = factor_of * jnp.repeat(draws, extent[position] // parts).reshape([-1 if axis == position else 1 for axis in range(len(extent))])
    return factor_of


def bell_draw(rng, extent, width, bound, pieces=(), kind=jnp.bfloat16):
    values = jax.random.normal(rng, extent, jnp.float32) * width
    if len(pieces) > 0:
        values = block_levels(rng, extent, pieces, -0.22, 0.18) * values
    return jnp.clip(values, min=-bound, max=bound).astype(kind)


def setup_inputs(seed: int = 0) -> dict:
    keys = jax.random.split(jax.random.key(seed), 6)
    return {
        "zonal_wind": bell_draw(keys[0], (LEVELS, NLAT, NLON), 1.0, 6.0, ((0, 8), (1, 32)), jnp.float32),
        "merid_wind": bell_draw(keys[1], (LEVELS, NLAT, NLON), 1.0, 6.0, ((0, 8), (1, 32)), jnp.float32),
        "tracer": bell_draw(keys[2], (LEVELS, NLAT, NLON), 1.0, 6.0, ((0, 8), (1, 32)), jnp.float32),
        "vertical_wind": bell_draw(keys[3], (LEVELS, NLAT, NLON), 1.0, 6.0, ((0, 8), (1, 32)), jnp.float32),
        "cutoff": draw_cutoff(jax.random.fold_in(keys[5], 71), 0),
    }


zonal_scale = 0.1
merid_scale = 0.1
vertical_scale = 0.1
highest = lax.Precision.HIGHEST


def mode_tables(first_mode, mode_count):
    point_ids = jnp.arange(NLON, dtype=jnp.int32)
    mode_ids = first_mode + jnp.arange(mode_count, dtype=jnp.int32)
    phase_ids = (point_ids[:, None] * mode_ids[None, :]) % NLON
    angles = phase_ids.astype(jnp.float32) * (2.0 * math.pi / NLON)
    return jnp.cos(angles), jnp.sin(angles)


def mode_weights(cut_rows, first_mode, mode_count):
    mode_ids = first_mode + jnp.arange(mode_count, dtype=jnp.int32)
    factor = jnp.where(mode_ids == 0, jnp.float32(1.0), jnp.float32(2.0)) / NLON
    return jnp.where(mode_ids[None, :] <= cut_rows[:, None], factor[None, :], jnp.float32(0.0))


def lowpass(fields, cut_rows, tables):
    summed = jnp.zeros_like(fields)
    for first_mode, cosines, sines in tables:
        weight = mode_weights(cut_rows, first_mode, cosines.shape[1])
        cosine_part = jnp.einsum("flan,nk->flak", fields, cosines, precision=highest, preferred_element_type=jnp.float32) * weight[None, None]
        sine_part = jnp.einsum("flan,nk->flak", fields, sines, precision=highest, preferred_element_type=jnp.float32) * weight[None, None]
        summed = summed + jnp.einsum("flak,nk->flan", cosine_part, cosines, precision=highest, preferred_element_type=jnp.float32)
        summed = summed + jnp.einsum("flak,nk->flan", sine_part, sines, precision=highest, preferred_element_type=jnp.float32)
    filtered_mask = (cut_rows < NLON // 2)[None, None, :, None]
    return jnp.where(filtered_mask, summed, fields)


def advect(field, zonal, merid, vertical):
    lat_rows = field.shape[1]
    east_wind = 0.5 * (zonal + jnp.roll(zonal, -1, axis=2))
    flux_x = zonal_scale * east_wind * (0.5 * (field + jnp.roll(field, -1, axis=2)))
    div_x = flux_x - jnp.roll(flux_x, 1, axis=2)
    face_ids = jnp.arange(lat_rows + 1, dtype=jnp.int32).astype(jnp.float32)
    face_cos = jnp.sin(face_ids * (math.pi / lat_rows))
    center_ids = jnp.arange(lat_rows, dtype=jnp.int32).astype(jnp.float32)
    center_cos = jnp.sin((center_ids + 0.5) * (math.pi / lat_rows))
    merid_lat = jnp.pad(merid, ((0, 0), (1, 1), (0, 0)))
    field_lat = jnp.pad(field, ((0, 0), (1, 1), (0, 0)))
    north_wind = 0.5 * (merid_lat[:, :-1] + merid_lat[:, 1:])
    flux_y = merid_scale * face_cos[None, :, None] * north_wind * (0.5 * (field_lat[:, :-1] + field_lat[:, 1:]))
    div_y = flux_y[:, 1:] - flux_y[:, :-1]
    vertical_pad = jnp.pad(vertical, ((1, 1), (0, 0), (0, 0)))
    field_lev = jnp.pad(field, ((1, 1), (0, 0), (0, 0)))
    upward = 0.5 * (vertical_pad[:-1] + vertical_pad[1:])
    flux_z = vertical_scale * upward * (0.5 * (field_lev[:-1] + field_lev[1:]))
    div_z = flux_z[1:] - flux_z[:-1]
    return field - (div_x + div_y) / center_cos[None, :, None] - div_z


def reference(zonal_wind, merid_wind, tracer, vertical_wind, cutoff):
    cosines, sines = mode_tables(0, KMAX)
    tables = [(0, cosines, sines)]
    stacked = jnp.stack([zonal_wind, merid_wind, tracer])
    south_rows = lowpass(stacked[:, :, :CAP], cutoff[:CAP], tables)
    north_rows = lowpass(stacked[:, :, NLAT - CAP:], cutoff[NLAT - CAP:], tables)
    filtered = jnp.concatenate([south_rows, stacked[:, :, CAP:NLAT - CAP], north_rows], axis=2)
    zonal_next = advect(filtered[0], filtered[0], filtered[1], vertical_wind)
    merid_next = advect(filtered[1], filtered[0], filtered[1], vertical_wind)
    tracer_next = advect(filtered[2], filtered[0], filtered[1], vertical_wind)
    return (zonal_next, merid_next, tracer_next)
```

```python
import math

import jax
import jax.numpy as jnp
from jax import lax
from jax.sharding import PartitionSpec as P

NLON = 2880
KMAX = 720
HALF = NLON // 2

zonal_scale = 0.1
merid_scale = 0.1
vertical_scale = 0.1
mxu_precision = lax.Precision.HIGH


def shift(x, axis, up):
    size = lax.axis_size(axis)
    pairs = [(i, i + 1) for i in range(size - 1)]
    if not up:
        pairs = [(j, i) for i, j in pairs]
    return lax.ppermute(x, axis, pairs)


def half_tables():
    point_ids = jnp.arange(HALF + 1, dtype=jnp.int32)
    mode_ids = jnp.arange(KMAX, dtype=jnp.int32)
    phase_ids = point_ids[:, None] * mode_ids[None, :] % NLON
    angles = phase_ids.astype(jnp.float32) * (2.0 * math.pi / NLON)
    return jnp.cos(angles), jnp.sin(angles)


def lowpass_rows(x, cut, cosines, sines):
    head = x[:, : HALF + 1]
    mirrored = jnp.concatenate([x[:, :1], jnp.flip(x[:, HALF:], axis=1)], axis=1)
    ends = jnp.ones((HALF + 1,), jnp.float32).at[0].set(0.5).at[HALF].set(0.5)
    even = (head + mirrored) * ends[None, :]
    odd = head - mirrored
    spec_cos = jnp.dot(even, cosines, precision=mxu_precision, preferred_element_type=jnp.float32)
    spec_sin = jnp.dot(odd, sines, precision=mxu_precision, preferred_element_type=jnp.float32)
    mode_ids = jnp.arange(KMAX, dtype=jnp.int32)
    factor = jnp.where(mode_ids == 0, jnp.float32(1.0), jnp.float32(2.0)) / NLON
    weight = jnp.where(mode_ids[None, :] <= cut[:, None], factor[None, :], jnp.float32(0.0))
    dims = (((1,), (1,)), ((), ()))
    even_out = lax.dot_general(spec_cos * weight, cosines, dims, precision=mxu_precision,
                               preferred_element_type=jnp.float32)
    odd_out = lax.dot_general(spec_sin * weight, sines, dims, precision=mxu_precision,
                              preferred_element_type=jnp.float32)
    first = even_out + odd_out
    second = jnp.flip((even_out - odd_out)[:, 1:HALF], axis=1)
    summed = jnp.concatenate([first, second], axis=1)
    return jnp.where((cut < HALF)[:, None], summed, x)


def filtered(x, cut, tables):
    shape = x.shape
    rows = x.reshape(-1, NLON)
    cuts = jnp.broadcast_to(cut, shape[:-1]).reshape(-1)
    out = lax.cond(jnp.any(cut < HALF), lambda: lowpass_rows(rows, cuts, *tables), lambda: rows)
    return out.reshape(shape)


def on_device(zonal_wind, merid_wind, tracer, vertical_wind, cutoff):
    lat_rows = zonal_wind.shape[1]
    lat_count = lax.axis_size("lat")
    lat_index = lax.axis_index("lat")
    total_rows = lat_rows * lat_count
    row_start = lat_index * lat_rows
    own_cut = lax.dynamic_slice_in_dim(cutoff, row_start, lat_rows)
    halo_ids = jnp.stack([row_start - 1, row_start + lat_rows])
    halo_cut = cutoff[jnp.clip(halo_ids, 0, total_rows - 1)]

    stacked = jnp.stack([zonal_wind, merid_wind, tracer])
    levels = stacked.shape[1]
    top = jnp.concatenate([stacked[:, levels - 1], vertical_wind[levels - 1 :]], axis=0)
    bottom = jnp.concatenate([stacked[:, 0], vertical_wind[:1]], axis=0)
    below = shift(top, "lev", True)
    above = shift(bottom, "lev", False)
    south = shift(stacked[:, :, lat_rows - 1 :], "lat", True)
    north = shift(stacked[:, :, :1], "lat", False)

    tables = half_tables()
    field = filtered(stacked, own_cut, tables)
    lat_halo = filtered(jnp.concatenate([south, north], axis=2), halo_cut, tables)
    lev_halo = filtered(jnp.stack([below[:3], above[:3]], axis=1), own_cut, tables)

    vertical_pad = jnp.concatenate([below[3:], vertical_wind, above[3:]], axis=0)
    field_lat = jnp.concatenate([lat_halo[:, :, :1], field, lat_halo[:, :, 1:]], axis=2)
    field_lev = jnp.concatenate([lev_halo[:, :1], field, lev_halo[:, 1:]], axis=1)

    face_ids = (row_start + jnp.arange(lat_rows + 1, dtype=jnp.int32)).astype(jnp.float32)
    face_cos = jnp.sin(face_ids * (math.pi / total_rows))
    center_ids = (row_start + jnp.arange(lat_rows, dtype=jnp.int32)).astype(jnp.float32)
    center_cos = jnp.sin((center_ids + 0.5) * (math.pi / total_rows))
    zonal_now = field[0]
    east_wind = 0.5 * (zonal_now + jnp.roll(zonal_now, -1, axis=2))
    flux_x = zonal_scale * east_wind[None] * (0.5 * (field + jnp.roll(field, -1, axis=3)))
    div_x = flux_x - jnp.roll(flux_x, 1, axis=3)
    merid_lat = field_lat[1]
    north_wind = 0.5 * (merid_lat[:, :-1] + merid_lat[:, 1:])
    flux_y = (
        merid_scale
        * face_cos[None, None, :, None]
        * north_wind[None]
        * (0.5 * (field_lat[:, :, :-1] + field_lat[:, :, 1:]))
    )
    div_y = flux_y[:, :, 1:] - flux_y[:, :, :-1]
    upward = 0.5 * (vertical_pad[:-1] + vertical_pad[1:])
    flux_z = vertical_scale * upward[None] * (0.5 * (field_lev[:, :-1] + field_lev[:, 1:]))
    div_z = flux_z[:, 1:] - flux_z[:, :-1]
    updated = field - (div_x + div_y) / center_cos[None, None, :, None] - div_z
    return (updated[0], updated[1], updated[2])


def solution(mesh):
    in_specs = (
        P("lev", "lat", None),
        P("lev", "lat", None),
        P("lev", "lat", None),
        P("lev", "lat", None),
        P(),
    )
    out_specs = (P("lev", "lat", None), P("lev", "lat", None), P("lev", "lat", None))
    return jax.shard_map(
        on_device, mesh=mesh, in_specs=in_specs, out_specs=out_specs, check_vma=False
    )
```

```python
import math

import jax
import numpy as np
import jax.numpy as jnp
from jax import lax
from jax.sharding import PartitionSpec as P

NLON = 2880
KMAX = 720
HALF = NLON // 2

zonal_scale = 0.1
merid_scale = 0.1
vertical_scale = 0.1
mxu_precision = lax.Precision.HIGH


def shift(x, axis, up):
    size = lax.axis_size(axis)
    pairs = [(i, i + 1) for i in range(size - 1)]
    if not up:
        pairs = [(j, i) for i, j in pairs]
    return lax.ppermute(x, axis, pairs)


def split_angles(modes):
    low = 48
    m_lo = np.arange(low)[:, None]
    m_hi = (low * np.arange(HALF // low))[:, None]
    k = np.asarray(modes)[None, :]
    step = 2.0 * np.pi / NLON
    lo = (m_lo * k) % NLON * step
    hi = (m_hi * k) % NLON * step
    as_f32 = lambda v: jnp.asarray(v.astype(np.float32))
    return as_f32(np.cos(lo)), as_f32(np.sin(lo)), as_f32(np.cos(hi)), as_f32(np.sin(hi))


def parity_table(parity):
    modes = np.arange(parity, KMAX, 2)
    cos_lo, sin_lo, cos_hi, sin_hi = split_angles(modes)
    cos_lo, sin_lo = cos_lo[None], sin_lo[None]
    cos_hi, sin_hi = cos_hi[:, None], sin_hi[:, None]
    cosines = cos_lo * cos_hi - sin_lo * sin_hi
    sines = sin_lo * cos_hi + cos_lo * sin_hi
    return jnp.concatenate([cosines, sines], axis=-1).reshape(HALF, KMAX)


def parity_weight(parity, cut):
    modes = np.arange(parity, KMAX, 2)
    mode_ids = jnp.asarray(np.concatenate([modes, modes]).astype(np.int32))
    factor = jnp.where(mode_ids == 0, jnp.float32(1.0), jnp.float32(2.0)) / NLON
    return jnp.where(mode_ids[None, :] <= cut[:, None], factor[None, :], jnp.float32(0.0))


def lowpass_rows(x, cut, tables):
    even_table, odd_table = tables
    first, second = x[:, :HALF], x[:, HALF:]
    spec_even = jnp.dot(first + second, even_table, precision=mxu_precision,
                        preferred_element_type=jnp.float32)
    spec_odd = jnp.dot(first - second, odd_table, precision=mxu_precision,
                       preferred_element_type=jnp.float32)
    dims = (((1,), (1,)), ((), ()))
    even_out = lax.dot_general(spec_even * parity_weight(0, cut), even_table, dims,
                               precision=mxu_precision, preferred_element_type=jnp.float32)
    odd_out = lax.dot_general(spec_odd * parity_weight(1, cut), odd_table, dims,
                              precision=mxu_precision, preferred_element_type=jnp.float32)
    summed = jnp.concatenate([even_out + odd_out, even_out - odd_out], axis=1)
    return jnp.where((cut < HALF)[:, None], summed, x)


def filtered(x, cut, tables):
    shape = x.shape
    rows = x.reshape(-1, NLON)
    cuts = jnp.broadcast_to(cut, shape[:-1]).reshape(-1)
    out = lax.cond(jnp.any(cut < HALF), lambda: lowpass_rows(rows, cuts, tables), lambda: rows)
    return out.reshape(shape)


def on_device(zonal_wind, merid_wind, tracer, vertical_wind, cutoff):
    lat_rows = zonal_wind.shape[1]
    lat_count = lax.axis_size("lat")
    lat_index = lax.axis_index("lat")
    total_rows = lat_rows * lat_count
    row_start = lat_index * lat_rows
    own_cut = lax.dynamic_slice_in_dim(cutoff, row_start, lat_rows)
    halo_ids = jnp.stack([row_start - 1, row_start + lat_rows])
    halo_cut = cutoff[jnp.clip(halo_ids, 0, total_rows - 1)]

    stacked = jnp.stack([zonal_wind, merid_wind, tracer])
    levels = stacked.shape[1]
    top = jnp.concatenate([stacked[:, levels - 1], vertical_wind[levels - 1 :]], axis=0)
    bottom = jnp.concatenate([stacked[:, 0], vertical_wind[:1]], axis=0)
    below = shift(top, "lev", True)
    above = shift(bottom, "lev", False)
    south = shift(stacked[:, :, lat_rows - 1 :], "lat", True)
    north = shift(stacked[:, :, :1], "lat", False)

    tables = (parity_table(0), parity_table(1))
    field = filtered(stacked, own_cut, tables)
    lat_rows_raw = jnp.concatenate([south, north], axis=2).reshape(-1, NLON)
    lev_rows_raw = jnp.stack([below[:3], above[:3]], axis=1).reshape(-1, NLON)
    lat_cuts = jnp.broadcast_to(halo_cut, south.shape[:2] + (2,)).reshape(-1)
    lev_cuts = jnp.broadcast_to(own_cut, (3, 2, lat_rows)).reshape(-1)
    halo_rows = filtered(jnp.concatenate([lat_rows_raw, lev_rows_raw]),
                         jnp.concatenate([lat_cuts, lev_cuts]), tables)
    lat_count_rows = lat_rows_raw.shape[0]
    lat_halo = halo_rows[:lat_count_rows].reshape(3, levels, 2, NLON)
    lev_halo = halo_rows[lat_count_rows:].reshape(3, 2, lat_rows, NLON)

    vertical_pad = jnp.concatenate([below[3:], vertical_wind, above[3:]], axis=0)
    field_lat = jnp.concatenate([lat_halo[:, :, :1], field, lat_halo[:, :, 1:]], axis=2)
    field_lev = jnp.concatenate([lev_halo[:, :1], field, lev_halo[:, 1:]], axis=1)

    face_ids = (row_start + jnp.arange(lat_rows + 1, dtype=jnp.int32)).astype(jnp.float32)
    face_cos = jnp.sin(face_ids * (math.pi / total_rows))
    center_ids = (row_start + jnp.arange(lat_rows, dtype=jnp.int32)).astype(jnp.float32)
    center_cos = jnp.sin((center_ids + 0.5) * (math.pi / total_rows))
    zonal_now = field[0]
    east_wind = 0.5 * (zonal_now + jnp.roll(zonal_now, -1, axis=2))
    flux_x = zonal_scale * east_wind[None] * (0.5 * (field + jnp.roll(field, -1, axis=3)))
    div_x = flux_x - jnp.roll(flux_x, 1, axis=3)
    merid_lat = field_lat[1]
    north_wind = 0.5 * (merid_lat[:, :-1] + merid_lat[:, 1:])
    flux_y = (
        merid_scale
        * face_cos[None, None, :, None]
        * north_wind[None]
        * (0.5 * (field_lat[:, :, :-1] + field_lat[:, :, 1:]))
    )
    div_y = flux_y[:, :, 1:] - flux_y[:, :, :-1]
    upward = 0.5 * (vertical_pad[:-1] + vertical_pad[1:])
    flux_z = vertical_scale * upward[None] * (0.5 * (field_lev[:, :-1] + field_lev[:, 1:]))
    div_z = flux_z[:, 1:] - flux_z[:, :-1]
    updated = field - (div_x + div_y) / center_cos[None, None, :, None] - div_z
    return (updated[0], updated[1], updated[2])


def solution(mesh):
    in_specs = (
        P("lev", "lat", None),
        P("lev", "lat", None),
        P("lev", "lat", None),
        P("lev", "lat", None),
        P(),
    )
    out_specs = (P("lev", "lat", None), P("lev", "lat", None), P("lev", "lat", None))
    return jax.shard_map(
        on_device, mesh=mesh, in_specs=in_specs, out_specs=out_specs, check_vma=False
    )
```

```python
import math

import jax
import numpy as np
import jax.numpy as jnp
from jax import lax
from jax.sharding import PartitionSpec as P

NLON = 2880
KMAX = 720
HALF = NLON // 2

zonal_scale = 0.1
merid_scale = 0.1
vertical_scale = 0.1
mxu_precision = lax.Precision.HIGH


def shift(x, axis, up):
    size = lax.axis_size(axis)
    pairs = [(i, i + 1) for i in range(size - 1)]
    if not up:
        pairs = [(j, i) for i, j in pairs]
    return lax.ppermute(x, axis, pairs)


def split_angles(modes):
    low = 48
    m_lo = np.arange(low)[:, None]
    m_hi = (low * np.arange(HALF // low))[:, None]
    k = np.asarray(modes)[None, :]
    step = 2.0 * np.pi / NLON
    lo = (m_lo * k) % NLON * step
    hi = (m_hi * k) % NLON * step
    as_f32 = lambda v: jnp.asarray(v.astype(np.float32))
    return as_f32(np.cos(lo)), as_f32(np.sin(lo)), as_f32(np.cos(hi)), as_f32(np.sin(hi))


def parity_table(parity):
    modes = np.arange(parity, KMAX, 2)
    cos_lo, sin_lo, cos_hi, sin_hi = split_angles(modes)
    cos_lo, sin_lo = cos_lo[None], sin_lo[None]
    cos_hi, sin_hi = cos_hi[:, None], sin_hi[:, None]
    cosines = cos_lo * cos_hi - sin_lo * sin_hi
    sines = sin_lo * cos_hi + cos_lo * sin_hi
    return jnp.concatenate([cosines, sines], axis=-1).reshape(HALF, KMAX)


def parity_weight(parity, cut):
    modes = np.arange(parity, KMAX, 2)
    mode_ids = jnp.asarray(np.concatenate([modes, modes]).astype(np.int32))
    factor = jnp.where(mode_ids == 0, jnp.float32(1.0), jnp.float32(2.0)) / NLON
    return jnp.where(mode_ids[None, :] <= cut[:, None], factor[None, :], jnp.float32(0.0))


def lowpass_rows(x, cut, tables):
    even_table, odd_table = tables
    first, second = x[:, :HALF], x[:, HALF:]
    forward = (((0,), (1,)), ((), ()))
    spec_even = lax.dot_general(even_table, first + second, forward, precision=mxu_precision,
                                preferred_element_type=jnp.float32)
    spec_odd = lax.dot_general(odd_table, first - second, forward, precision=mxu_precision,
                               preferred_element_type=jnp.float32)
    inverse = (((0,), (1,)), ((), ()))
    even_out = lax.dot_general(spec_even * parity_weight(0, cut).T, even_table, inverse,
                               precision=mxu_precision, preferred_element_type=jnp.float32)
    odd_out = lax.dot_general(spec_odd * parity_weight(1, cut).T, odd_table, inverse,
                              precision=mxu_precision, preferred_element_type=jnp.float32)
    summed = jnp.concatenate([even_out + odd_out, even_out - odd_out], axis=1)
    return jnp.where((cut < HALF)[:, None], summed, x)


def filtered(x, cut, tables):
    shape = x.shape
    rows = x.reshape(-1, NLON)
    cuts = jnp.broadcast_to(cut, shape[:-1]).reshape(-1)
    out = lax.cond(jnp.any(cut < HALF), lambda: lowpass_rows(rows, cuts, tables), lambda: rows)
    return out.reshape(shape)


def on_device(zonal_wind, merid_wind, tracer, vertical_wind, cutoff):
    lat_rows = zonal_wind.shape[1]
    lat_count = lax.axis_size("lat")
    lat_index = lax.axis_index("lat")
    total_rows = lat_rows * lat_count
    row_start = lat_index * lat_rows
    own_cut = lax.dynamic_slice_in_dim(cutoff, row_start, lat_rows)
    halo_ids = jnp.stack([row_start - 1, row_start + lat_rows])
    halo_cut = cutoff[jnp.clip(halo_ids, 0, total_rows - 1)]

    stacked = jnp.stack([zonal_wind, merid_wind, tracer])
    levels = stacked.shape[1]
    top = jnp.concatenate([stacked[:, levels - 1], vertical_wind[levels - 1 :]], axis=0)
    bottom = jnp.concatenate([stacked[:, 0], vertical_wind[:1]], axis=0)
    below = shift(top, "lev", True)
    above = shift(bottom, "lev", False)
    south = shift(stacked[:, :, lat_rows - 1 :], "lat", True)
    north = shift(stacked[:, :, :1], "lat", False)

    tables = (parity_table(0), parity_table(1))
    field = filtered(stacked, own_cut, tables)
    lat_rows_raw = jnp.concatenate([south, north], axis=2).reshape(-1, NLON)
    lev_rows_raw = jnp.stack([below[:3], above[:3]], axis=1).reshape(-1, NLON)
    lat_cuts = jnp.broadcast_to(halo_cut, south.shape[:2] + (2,)).reshape(-1)
    lev_cuts = jnp.broadcast_to(own_cut, (3, 2, lat_rows)).reshape(-1)
    halo_rows = filtered(jnp.concatenate([lat_rows_raw, lev_rows_raw]),
                         jnp.concatenate([lat_cuts, lev_cuts]), tables)
    lat_count_rows = lat_rows_raw.shape[0]
    lat_halo = halo_rows[:lat_count_rows].reshape(3, levels, 2, NLON)
    lev_halo = halo_rows[lat_count_rows:].reshape(3, 2, lat_rows, NLON)

    vertical_pad = jnp.concatenate([below[3:], vertical_wind, above[3:]], axis=0)
    field_lat = jnp.concatenate([lat_halo[:, :, :1], field, lat_halo[:, :, 1:]], axis=2)
    field_lev = jnp.concatenate([lev_halo[:, :1], field, lev_halo[:, 1:]], axis=1)

    face_ids = (row_start + jnp.arange(lat_rows + 1, dtype=jnp.int32)).astype(jnp.float32)
    face_cos = jnp.sin(face_ids * (math.pi / total_rows))
    center_ids = (row_start + jnp.arange(lat_rows, dtype=jnp.int32)).astype(jnp.float32)
    center_cos = jnp.sin((center_ids + 0.5) * (math.pi / total_rows))
    zonal_now = field[0]
    east_wind = 0.5 * (zonal_now + jnp.roll(zonal_now, -1, axis=2))
    flux_x = zonal_scale * east_wind[None] * (0.5 * (field + jnp.roll(field, -1, axis=3)))
    div_x = flux_x - jnp.roll(flux_x, 1, axis=3)
    merid_lat = field_lat[1]
    north_wind = 0.5 * (merid_lat[:, :-1] + merid_lat[:, 1:])
    flux_y = (
        merid_scale
        * face_cos[None, None, :, None]
        * north_wind[None]
        * (0.5 * (field_lat[:, :, :-1] + field_lat[:, :, 1:]))
    )
    div_y = flux_y[:, :, 1:] - flux_y[:, :, :-1]
    upward = 0.5 * (vertical_pad[:-1] + vertical_pad[1:])
    flux_z = vertical_scale * upward[None] * (0.5 * (field_lev[:, :-1] + field_lev[:, 1:]))
    div_z = flux_z[:, 1:] - flux_z[:, :-1]
    updated = field - (div_x + div_y) / center_cos[None, None, :, None] - div_z
    return (updated[0], updated[1], updated[2])


def solution(mesh):
    in_specs = (
        P("lev", "lat", None),
        P("lev", "lat", None),
        P("lev", "lat", None),
        P("lev", "lat", None),
        P(),
    )
    out_specs = (P("lev", "lat", None), P("lev", "lat", None), P("lev", "lat", None))
    return jax.shard_map(
        on_device, mesh=mesh, in_specs=in_specs, out_specs=out_specs, check_vma=False
    )
```

```python
import math

import jax
import numpy as np
import jax.numpy as jnp
from jax import lax
from jax.sharding import PartitionSpec as P

NLON = 2880
KMAX = 720
HALF = NLON // 2

zonal_scale = 0.1
merid_scale = 0.1
vertical_scale = 0.1
mxu_precision = lax.Precision.HIGH


def shift(x, axis, up):
    size = lax.axis_size(axis)
    pairs = [(i, i + 1) for i in range(size - 1)]
    if not up:
        pairs = [(j, i) for i, j in pairs]
    return lax.ppermute(x, axis, pairs)


def split_angles(modes):
    low = 48
    m_lo = np.arange(low)[:, None]
    m_hi = (low * np.arange(HALF // low))[:, None]
    k = np.asarray(modes)[None, :]
    step = 2.0 * np.pi / NLON
    lo = (m_lo * k) % NLON * step
    hi = (m_hi * k) % NLON * step
    as_f32 = lambda v: jnp.asarray(v.astype(np.float32))
    return as_f32(np.cos(lo)), as_f32(np.sin(lo)), as_f32(np.cos(hi)), as_f32(np.sin(hi))


def parity_table(parity):
    modes = np.arange(parity, KMAX, 2)
    cos_lo, sin_lo, cos_hi, sin_hi = split_angles(modes)
    cos_lo, sin_lo = cos_lo[None], sin_lo[None]
    cos_hi, sin_hi = cos_hi[:, None], sin_hi[:, None]
    cosines = cos_lo * cos_hi - sin_lo * sin_hi
    sines = sin_lo * cos_hi + cos_lo * sin_hi
    return jnp.concatenate([cosines, sines], axis=-1).reshape(HALF, KMAX)


def parity_weight(parity, cut):
    modes = np.arange(parity, KMAX, 2)
    mode_ids = jnp.asarray(np.concatenate([modes, modes]).astype(np.int32))
    factor = jnp.where(mode_ids == 0, jnp.float32(1.0), jnp.float32(2.0)) / NLON
    return jnp.where(mode_ids[None, :] <= cut[:, None], factor[None, :], jnp.float32(0.0))


def lowpass_rows(x, cut, tables):
    even_table, odd_table = tables
    first, second = x[:, :HALF], x[:, HALF:]
    spec_even = jnp.dot(first + second, even_table, precision=mxu_precision,
                        preferred_element_type=jnp.float32)
    spec_odd = jnp.dot(first - second, odd_table, precision=mxu_precision,
                       preferred_element_type=jnp.float32)
    dims = (((1,), (1,)), ((), ()))
    even_out = lax.dot_general(spec_even * parity_weight(0, cut), even_table, dims,
                               precision=mxu_precision, preferred_element_type=jnp.float32)
    odd_out = lax.dot_general(spec_odd * parity_weight(1, cut), odd_table, dims,
                              precision=mxu_precision, preferred_element_type=jnp.float32)
    summed = jnp.concatenate([even_out + odd_out, even_out - odd_out], axis=1)
    return jnp.where((cut < HALF)[:, None], summed, x)


def filtered(x, cut, tables):
    shape = x.shape
    rows = x.reshape(-1, NLON)
    cuts = jnp.broadcast_to(cut, shape[:-1]).reshape(-1)
    out = lax.cond(jnp.any(cut < HALF), lambda: lowpass_rows(rows, cuts, tables), lambda: rows)
    return out.reshape(shape)


def on_device(zonal_wind, merid_wind, tracer, vertical_wind, cutoff):
    lat_rows = zonal_wind.shape[1]
    lat_count = lax.axis_size("lat")
    lat_index = lax.axis_index("lat")
    total_rows = lat_rows * lat_count
    row_start = lat_index * lat_rows
    own_cut = lax.dynamic_slice_in_dim(cutoff, row_start, lat_rows)
    halo_ids = jnp.stack([row_start - 1, row_start + lat_rows])
    halo_cut = cutoff[jnp.clip(halo_ids, 0, total_rows - 1)]

    stacked = jnp.stack([zonal_wind, merid_wind, tracer])
    levels = stacked.shape[1]
    below_fields = shift(stacked[:, levels - 1], "lev", True)
    above_fields = shift(stacked[:, 0], "lev", False)
    top_wind, bottom_wind, _ = lax.optimization_barrier(
        (vertical_wind[levels - 1 :], vertical_wind[:1], (below_fields, above_fields)))
    below_wind = shift(top_wind, "lev", True)
    above_wind = shift(bottom_wind, "lev", False)
    south = shift(stacked[:, :, lat_rows - 1 :], "lat", True)
    north = shift(stacked[:, :, :1], "lat", False)

    tables = (parity_table(0), parity_table(1))
    field = filtered(stacked, own_cut, tables)
    lat_rows_raw = jnp.concatenate([south, north], axis=2).reshape(-1, NLON)
    lev_rows_raw = jnp.stack([below_fields, above_fields], axis=1).reshape(-1, NLON)
    lat_cuts = jnp.broadcast_to(halo_cut, south.shape[:2] + (2,)).reshape(-1)
    lev_cuts = jnp.broadcast_to(own_cut, (3, 2, lat_rows)).reshape(-1)
    halo_rows = filtered(jnp.concatenate([lat_rows_raw, lev_rows_raw]),
                         jnp.concatenate([lat_cuts, lev_cuts]), tables)
    lat_count_rows = lat_rows_raw.shape[0]
    lat_halo = halo_rows[:lat_count_rows].reshape(3, levels, 2, NLON)
    lev_halo = halo_rows[lat_count_rows:].reshape(3, 2, lat_rows, NLON)

    vertical_pad = jnp.concatenate([below_wind, vertical_wind, above_wind], axis=0)
    field_lat = jnp.concatenate([lat_halo[:, :, :1], field, lat_halo[:, :, 1:]], axis=2)
    field_lev = jnp.concatenate([lev_halo[:, :1], field, lev_halo[:, 1:]], axis=1)

    face_ids = (row_start + jnp.arange(lat_rows + 1, dtype=jnp.int32)).astype(jnp.float32)
    face_cos = jnp.sin(face_ids * (math.pi / total_rows))
    center_ids = (row_start + jnp.arange(lat_rows, dtype=jnp.int32)).astype(jnp.float32)
    center_cos = jnp.sin((center_ids + 0.5) * (math.pi / total_rows))
    zonal_now = field[0]
    east_wind = 0.5 * (zonal_now + jnp.roll(zonal_now, -1, axis=2))
    flux_x = zonal_scale * east_wind[None] * (0.5 * (field + jnp.roll(field, -1, axis=3)))
    div_x = flux_x - jnp.roll(flux_x, 1, axis=3)
    merid_lat = field_lat[1]
    north_wind = 0.5 * (merid_lat[:, :-1] + merid_lat[:, 1:])
    flux_y = (
        merid_scale
        * face_cos[None, None, :, None]
        * north_wind[None]
        * (0.5 * (field_lat[:, :, :-1] + field_lat[:, :, 1:]))
    )
    div_y = flux_y[:, :, 1:] - flux_y[:, :, :-1]
    upward = 0.5 * (vertical_pad[:-1] + vertical_pad[1:])
    flux_z = vertical_scale * upward[None] * (0.5 * (field_lev[:, :-1] + field_lev[:, 1:]))
    div_z = flux_z[:, 1:] - flux_z[:, :-1]
    updated = field - (div_x + div_y) / center_cos[None, None, :, None] - div_z
    return (updated[0], updated[1], updated[2])


def solution(mesh):
    in_specs = (
        P("lev", "lat", None),
        P("lev", "lat", None),
        P("lev", "lat", None),
        P("lev", "lat", None),
        P(),
    )
    out_specs = (P("lev", "lat", None), P("lev", "lat", None), P("lev", "lat", None))
    return jax.shard_map(
        on_device, mesh=mesh, in_specs=in_specs, out_specs=out_specs, check_vma=False
    )
```

```python
import math

import jax
import numpy as np
import jax.numpy as jnp
from jax import lax
from jax.sharding import PartitionSpec as P

NLON = 2880
KMAX = 720
HALF = NLON // 2

zonal_scale = 0.1
merid_scale = 0.1
vertical_scale = 0.1
mxu_precision = lax.Precision.HIGH


def shift(x, axis, up):
    size = lax.axis_size(axis)
    pairs = [(i, i + 1) for i in range(size - 1)]
    if not up:
        pairs = [(j, i) for i, j in pairs]
    return lax.ppermute(x, axis, pairs)


def split_angles(modes):
    low = 48
    m_lo = np.arange(low)[:, None]
    m_hi = (low * np.arange(HALF // low))[:, None]
    k = np.asarray(modes)[None, :]
    step = 2.0 * np.pi / NLON
    lo = (m_lo * k) % NLON * step
    hi = (m_hi * k) % NLON * step
    as_f32 = lambda v: jnp.asarray(v.astype(np.float32))
    return as_f32(np.cos(lo)), as_f32(np.sin(lo)), as_f32(np.cos(hi)), as_f32(np.sin(hi))


def parity_table(parity):
    modes = np.arange(parity, KMAX, 2)
    cos_lo, sin_lo, cos_hi, sin_hi = split_angles(modes)
    cos_lo, sin_lo = cos_lo[None], sin_lo[None]
    cos_hi, sin_hi = cos_hi[:, None], sin_hi[:, None]
    cosines = cos_lo * cos_hi - sin_lo * sin_hi
    sines = sin_lo * cos_hi + cos_lo * sin_hi
    return jnp.concatenate([cosines, sines], axis=-1).reshape(HALF, KMAX)


def parity_weight(parity, cut):
    modes = np.arange(parity, KMAX, 2)
    mode_ids = jnp.asarray(np.concatenate([modes, modes]).astype(np.int32))
    factor = jnp.where(mode_ids == 0, jnp.float32(1.0), jnp.float32(2.0)) / NLON
    return jnp.where(mode_ids[None, :] <= cut[:, None], factor[None, :], jnp.float32(0.0))


def lowpass_rows(x, cut, tables):
    even_table, odd_table = tables
    first, second = x[:, :HALF], x[:, HALF:]
    spec_even = jnp.dot(first + second, even_table, precision=mxu_precision,
                        preferred_element_type=jnp.float32)
    spec_odd = jnp.dot(first - second, odd_table, precision=mxu_precision,
                       preferred_element_type=jnp.float32)
    dims = (((1,), (1,)), ((), ()))
    even_out = lax.dot_general(spec_even * parity_weight(0, cut), even_table, dims,
                               precision=mxu_precision, preferred_element_type=jnp.float32)
    odd_out = lax.dot_general(spec_odd * parity_weight(1, cut), odd_table, dims,
                              precision=mxu_precision, preferred_element_type=jnp.float32)
    summed = jnp.concatenate([even_out + odd_out, even_out - odd_out], axis=1)
    return jnp.where((cut < HALF)[:, None], summed, x)


def filtered(x, cut, tables):
    shape = x.shape
    rows = x.reshape(-1, NLON)
    cuts = jnp.broadcast_to(cut, shape[:-1]).reshape(-1)
    out = lax.cond(jnp.any(cut < HALF), lambda: lowpass_rows(rows, cuts, tables), lambda: rows)
    return out.reshape(shape)


def on_device(zonal_wind, merid_wind, tracer, vertical_wind, cutoff):
    lat_rows = zonal_wind.shape[1]
    lat_count = lax.axis_size("lat")
    lat_index = lax.axis_index("lat")
    total_rows = lat_rows * lat_count
    row_start = lat_index * lat_rows
    own_cut = lax.dynamic_slice_in_dim(cutoff, row_start, lat_rows)

    stacked = jnp.stack([zonal_wind, merid_wind, tracer])
    levels = stacked.shape[1]
    below_wind = shift(vertical_wind[levels - 1 :], "lev", True)
    above_wind = shift(vertical_wind[:1], "lev", False)

    tables = (parity_table(0), parity_table(1))
    stacked, below_wind, above_wind = lax.optimization_barrier((stacked, below_wind, above_wind))
    field = filtered(stacked, own_cut, tables)
    below = shift(field[:, levels - 1 :], "lev", True)
    above = shift(field[:, :1], "lev", False)
    south = shift(field[:, :, lat_rows - 1 :], "lat", True)
    north = shift(field[:, :, :1], "lat", False)

    vertical_pad = jnp.concatenate([below_wind, vertical_wind, above_wind], axis=0)
    field_lat = jnp.concatenate([south, field, north], axis=2)
    field_lev = jnp.concatenate([below, field, above], axis=1)

    face_ids = (row_start + jnp.arange(lat_rows + 1, dtype=jnp.int32)).astype(jnp.float32)
    face_cos = jnp.sin(face_ids * (math.pi / total_rows))
    center_ids = (row_start + jnp.arange(lat_rows, dtype=jnp.int32)).astype(jnp.float32)
    center_cos = jnp.sin((center_ids + 0.5) * (math.pi / total_rows))
    zonal_now = field[0]
    east_wind = 0.5 * (zonal_now + jnp.roll(zonal_now, -1, axis=2))
    flux_x = zonal_scale * east_wind[None] * (0.5 * (field + jnp.roll(field, -1, axis=3)))
    div_x = flux_x - jnp.roll(flux_x, 1, axis=3)
    merid_lat = field_lat[1]
    north_wind = 0.5 * (merid_lat[:, :-1] + merid_lat[:, 1:])
    flux_y = (
        merid_scale
        * face_cos[None, None, :, None]
        * north_wind[None]
        * (0.5 * (field_lat[:, :, :-1] + field_lat[:, :, 1:]))
    )
    div_y = flux_y[:, :, 1:] - flux_y[:, :, :-1]
    upward = 0.5 * (vertical_pad[:-1] + vertical_pad[1:])
    flux_z = vertical_scale * upward[None] * (0.5 * (field_lev[:, :-1] + field_lev[:, 1:]))
    div_z = flux_z[:, 1:] - flux_z[:, :-1]
    updated = field - (div_x + div_y) / center_cos[None, None, :, None] - div_z
    return (updated[0], updated[1], updated[2])


def solution(mesh):
    in_specs = (
        P("lev", "lat", None),
        P("lev", "lat", None),
        P("lev", "lat", None),
        P("lev", "lat", None),
        P(),
    )
    out_specs = (P("lev", "lat", None), P("lev", "lat", None), P("lev", "lat", None))
    return jax.shard_map(
        on_device, mesh=mesh, in_specs=in_specs, out_specs=out_specs, check_vma=False
    )
```

```python
import math

import jax
import numpy as np
import jax.numpy as jnp
from jax import lax
from jax.sharding import PartitionSpec as P

NLON = 2880
KMAX = 720
HALF = NLON // 2
CAP = 80

zonal_scale = 0.1
merid_scale = 0.1
vertical_scale = 0.1
mxu_precision = lax.Precision.HIGH


def shift(x, axis, up):
    size = lax.axis_size(axis)
    pairs = [(i, i + 1) for i in range(size - 1)]
    if not up:
        pairs = [(j, i) for i, j in pairs]
    return lax.ppermute(x, axis, pairs)


def group_shift(x, lat_group, up):
    lev_size = lax.axis_size("lev")
    pairs = []
    for lat in lat_group:
        for lev in range(lev_size - 1):
            source, target = lat * lev_size + lev, lat * lev_size + lev + 1
            pairs.append((source, target) if up else (target, source))
    return lax.ppermute(x, ("lat", "lev"), pairs)


def split_angles(modes):
    low = 48
    m_lo = np.arange(low)[:, None]
    m_hi = (low * np.arange(HALF // low))[:, None]
    k = np.asarray(modes)[None, :]
    step = 2.0 * np.pi / NLON
    lo = (m_lo * k) % NLON * step
    hi = (m_hi * k) % NLON * step
    as_f32 = lambda v: jnp.asarray(v.astype(np.float32))
    return as_f32(np.cos(lo)), as_f32(np.sin(lo)), as_f32(np.cos(hi)), as_f32(np.sin(hi))


def parity_table(parity):
    modes = np.arange(parity, KMAX, 2)
    cos_lo, sin_lo, cos_hi, sin_hi = split_angles(modes)
    cos_lo, sin_lo = cos_lo[None], sin_lo[None]
    cos_hi, sin_hi = cos_hi[:, None], sin_hi[:, None]
    cosines = cos_lo * cos_hi - sin_lo * sin_hi
    sines = sin_lo * cos_hi + cos_lo * sin_hi
    return jnp.concatenate([cosines, sines], axis=-1).reshape(HALF, KMAX)


def parity_weight(parity, cut):
    modes = np.arange(parity, KMAX, 2)
    mode_ids = jnp.asarray(np.concatenate([modes, modes]).astype(np.int32))
    factor = jnp.where(mode_ids == 0, jnp.float32(1.0), jnp.float32(2.0)) / NLON
    return jnp.where(mode_ids[None, :] <= cut[:, None], factor[None, :], jnp.float32(0.0))


def lowpass_rows(x, cut, tables):
    even_table, odd_table = tables
    first, second = x[:, :HALF], x[:, HALF:]
    spec_even = jnp.dot(first + second, even_table, precision=mxu_precision,
                        preferred_element_type=jnp.float32)
    spec_odd = jnp.dot(first - second, odd_table, precision=mxu_precision,
                       preferred_element_type=jnp.float32)
    dims = (((1,), (1,)), ((), ()))
    even_out = lax.dot_general(spec_even * parity_weight(0, cut), even_table, dims,
                               precision=mxu_precision, preferred_element_type=jnp.float32)
    odd_out = lax.dot_general(spec_odd * parity_weight(1, cut), odd_table, dims,
                              precision=mxu_precision, preferred_element_type=jnp.float32)
    summed = jnp.concatenate([even_out + odd_out, even_out - odd_out], axis=1)
    return jnp.where((cut < HALF)[:, None], summed, x)


def filtered(x, cut, tables):
    shape = x.shape
    rows = x.reshape(-1, NLON)
    cuts = jnp.broadcast_to(cut, shape[:-1]).reshape(-1)
    out = lax.cond(jnp.any(cut < HALF), lambda: lowpass_rows(rows, cuts, tables), lambda: rows)
    return out.reshape(shape)


def on_device(zonal_wind, merid_wind, tracer, vertical_wind, cutoff):
    lat_rows = zonal_wind.shape[1]
    lat_count = lax.axis_size("lat")
    lat_index = lax.axis_index("lat")
    total_rows = lat_rows * lat_count
    row_start = lat_index * lat_rows
    own_cut = lax.dynamic_slice_in_dim(cutoff, row_start, lat_rows)

    stacked = jnp.stack([zonal_wind, merid_wind, tracer])
    levels = stacked.shape[1]
    pole_rows = [min(j, total_rows - 1 - j) + 1 <= CAP for j in range(total_rows)]
    filter_lat = [i for i in range(lat_count) if any(pole_rows[i * lat_rows:(i + 1) * lat_rows])]
    plain_lat = [i for i in range(lat_count) if i not in filter_lat]
    below_wind = shift(vertical_wind[levels - 1 :], "lev", True)
    above_wind = shift(vertical_wind[:1], "lev", False)
    below_plain = group_shift(stacked[:, levels - 1 :], plain_lat, True)
    above_plain = group_shift(stacked[:, :1], plain_lat, False)

    tables = (parity_table(0), parity_table(1))
    stacked, below_wind, above_wind, below_plain, above_plain = lax.optimization_barrier(
        (stacked, below_wind, above_wind, below_plain, above_plain))
    field = filtered(stacked, own_cut, tables)
    below_filtered = group_shift(field[:, levels - 1 :], filter_lat, True)
    above_filtered = group_shift(field[:, :1], filter_lat, False)
    is_filter = jnp.any(lat_index == jnp.asarray(filter_lat, jnp.int32))
    below = jnp.where(is_filter, below_filtered, below_plain)
    above = jnp.where(is_filter, above_filtered, above_plain)
    south = shift(field[:, :, lat_rows - 1 :], "lat", True)
    north = shift(field[:, :, :1], "lat", False)

    vertical_pad = jnp.concatenate([below_wind, vertical_wind, above_wind], axis=0)
    field_lat = jnp.concatenate([south, field, north], axis=2)
    field_lev = jnp.concatenate([below, field, above], axis=1)

    face_ids = (row_start + jnp.arange(lat_rows + 1, dtype=jnp.int32)).astype(jnp.float32)
    face_cos = jnp.sin(face_ids * (math.pi / total_rows))
    center_ids = (row_start + jnp.arange(lat_rows, dtype=jnp.int32)).astype(jnp.float32)
    center_cos = jnp.sin((center_ids + 0.5) * (math.pi / total_rows))
    zonal_now = field[0]
    east_wind = 0.5 * (zonal_now + jnp.roll(zonal_now, -1, axis=2))
    flux_x = zonal_scale * east_wind[None] * (0.5 * (field + jnp.roll(field, -1, axis=3)))
    div_x = flux_x - jnp.roll(flux_x, 1, axis=3)
    merid_lat = field_lat[1]
    north_wind = 0.5 * (merid_lat[:, :-1] + merid_lat[:, 1:])
    flux_y = (
        merid_scale
        * face_cos[None, None, :, None]
        * north_wind[None]
        * (0.5 * (field_lat[:, :, :-1] + field_lat[:, :, 1:]))
    )
    div_y = flux_y[:, :, 1:] - flux_y[:, :, :-1]
    upward = 0.5 * (vertical_pad[:-1] + vertical_pad[1:])
    flux_z = vertical_scale * upward[None] * (0.5 * (field_lev[:, :-1] + field_lev[:, 1:]))
    div_z = flux_z[:, 1:] - flux_z[:, :-1]
    updated = field - (div_x + div_y) / center_cos[None, None, :, None] - div_z
    return (updated[0], updated[1], updated[2])


def solution(mesh):
    in_specs = (
        P("lev", "lat", None),
        P("lev", "lat", None),
        P("lev", "lat", None),
        P("lev", "lat", None),
        P(),
    )
    out_specs = (P("lev", "lat", None), P("lev", "lat", None), P("lev", "lat", None))
    return jax.shard_map(
        on_device, mesh=mesh, in_specs=in_specs, out_specs=out_specs, check_vma=False
    )
```

```python
import math

import jax
import numpy as np
import jax.numpy as jnp
from jax import lax
from jax.sharding import PartitionSpec as P

NLON = 2880
KMAX = 720
HALF = NLON // 2
CAP = 80

zonal_scale = 0.1
merid_scale = 0.1
vertical_scale = 0.1
mxu_precision = lax.Precision.HIGH


def shift(x, axis, up):
    size = lax.axis_size(axis)
    pairs = [(i, i + 1) for i in range(size - 1)]
    if not up:
        pairs = [(j, i) for i, j in pairs]
    return lax.ppermute(x, axis, pairs)


def group_shift(x, lat_group, up):
    lev_size = lax.axis_size("lev")
    pairs = []
    for lat in lat_group:
        for lev in range(lev_size - 1):
            source, target = lat * lev_size + lev, lat * lev_size + lev + 1
            pairs.append((source, target) if up else (target, source))
    return lax.ppermute(x, ("lat", "lev"), pairs)


def split_angles(modes):
    low = 48
    m_lo = np.arange(low)[:, None]
    m_hi = (low * np.arange(HALF // low))[:, None]
    k = np.asarray(modes)[None, :]
    step = 2.0 * np.pi / NLON
    lo = (m_lo * k) % NLON * step
    hi = (m_hi * k) % NLON * step
    as_f32 = lambda v: jnp.asarray(v.astype(np.float32))
    return as_f32(np.cos(lo)), as_f32(np.sin(lo)), as_f32(np.cos(hi)), as_f32(np.sin(hi))


def parity_table(parity):
    modes = np.arange(parity, KMAX, 2)
    cos_lo, sin_lo, cos_hi, sin_hi = split_angles(modes)
    cos_lo, sin_lo = cos_lo[None], sin_lo[None]
    cos_hi, sin_hi = cos_hi[:, None], sin_hi[:, None]
    cosines = cos_lo * cos_hi - sin_lo * sin_hi
    sines = sin_lo * cos_hi + cos_lo * sin_hi
    return jnp.concatenate([cosines, sines], axis=-1).reshape(HALF, KMAX)


def parity_weight(parity, cut):
    modes = np.arange(parity, KMAX, 2)
    mode_ids = jnp.asarray(np.concatenate([modes, modes]).astype(np.int32))
    factor = jnp.where(mode_ids == 0, jnp.float32(1.0), jnp.float32(2.0)) / NLON
    return jnp.where(mode_ids[None, :] <= cut[:, None], factor[None, :], jnp.float32(0.0))


def lowpass_rows(x, cut, tables):
    even_table, odd_table = tables
    first, second = x[:, :HALF], x[:, HALF:]
    spec_even = jnp.dot(first + second, even_table, precision=mxu_precision,
                        preferred_element_type=jnp.float32)
    spec_odd = jnp.dot(first - second, odd_table, precision=mxu_precision,
                       preferred_element_type=jnp.float32)
    dims = (((1,), (1,)), ((), ()))
    even_out = lax.dot_general(spec_even * parity_weight(0, cut), even_table, dims,
                               precision=mxu_precision, preferred_element_type=jnp.float32)
    odd_out = lax.dot_general(spec_odd * parity_weight(1, cut), odd_table, dims,
                              precision=mxu_precision, preferred_element_type=jnp.float32)
    summed = jnp.concatenate([even_out + odd_out, even_out - odd_out], axis=1)
    return jnp.where((cut < HALF)[:, None], summed, x)


def filtered(x, cut, tables):
    shape = x.shape
    rows = x.reshape(-1, NLON)
    cuts = jnp.broadcast_to(cut, shape[:-1]).reshape(-1)
    out = lax.cond(jnp.any(cut < HALF), lambda: lowpass_rows(rows, cuts, tables), lambda: rows)
    return out.reshape(shape)


def on_device(zonal_wind, merid_wind, tracer, vertical_wind, cutoff):
    lat_rows = zonal_wind.shape[1]
    lat_count = lax.axis_size("lat")
    lat_index = lax.axis_index("lat")
    total_rows = lat_rows * lat_count
    row_start = lat_index * lat_rows
    own_cut = lax.dynamic_slice_in_dim(cutoff, row_start, lat_rows)

    stacked = jnp.stack([zonal_wind, merid_wind, tracer])
    levels = stacked.shape[1]
    pole_rows = [min(j, total_rows - 1 - j) + 1 <= CAP for j in range(total_rows)]
    filter_lat = [i for i in range(lat_count) if any(pole_rows[i * lat_rows:(i + 1) * lat_rows])]
    plain_lat = [i for i in range(lat_count) if i not in filter_lat]
    below_plain = group_shift(stacked[:, levels - 1 :], plain_lat, True)
    above_plain = group_shift(stacked[:, :1], plain_lat, False)

    tables = (parity_table(0), parity_table(1))
    stacked, below_plain, above_plain = lax.optimization_barrier((stacked, below_plain, above_plain))
    field = filtered(stacked, own_cut, tables)
    top_wind, bottom_wind, field = lax.optimization_barrier(
        (vertical_wind[levels - 1 :], vertical_wind[:1], field))
    below_wind = shift(top_wind, "lev", True)
    above_wind = shift(bottom_wind, "lev", False)
    below_filtered = group_shift(field[:, levels - 1 :], filter_lat, True)
    above_filtered = group_shift(field[:, :1], filter_lat, False)
    is_filter = jnp.any(lat_index == jnp.asarray(filter_lat, jnp.int32))
    below = jnp.where(is_filter, below_filtered, below_plain)
    above = jnp.where(is_filter, above_filtered, above_plain)
    south = shift(field[:, :, lat_rows - 1 :], "lat", True)
    north = shift(field[:, :, :1], "lat", False)

    vertical_pad = jnp.concatenate([below_wind, vertical_wind, above_wind], axis=0)
    field_lat = jnp.concatenate([south, field, north], axis=2)
    field_lev = jnp.concatenate([below, field, above], axis=1)

    face_ids = (row_start + jnp.arange(lat_rows + 1, dtype=jnp.int32)).astype(jnp.float32)
    face_cos = jnp.sin(face_ids * (math.pi / total_rows))
    center_ids = (row_start + jnp.arange(lat_rows, dtype=jnp.int32)).astype(jnp.float32)
    center_cos = jnp.sin((center_ids + 0.5) * (math.pi / total_rows))
    zonal_now = field[0]
    east_wind = 0.5 * (zonal_now + jnp.roll(zonal_now, -1, axis=2))
    flux_x = zonal_scale * east_wind[None] * (0.5 * (field + jnp.roll(field, -1, axis=3)))
    div_x = flux_x - jnp.roll(flux_x, 1, axis=3)
    merid_lat = field_lat[1]
    north_wind = 0.5 * (merid_lat[:, :-1] + merid_lat[:, 1:])
    flux_y = (
        merid_scale
        * face_cos[None, None, :, None]
        * north_wind[None]
        * (0.5 * (field_lat[:, :, :-1] + field_lat[:, :, 1:]))
    )
    div_y = flux_y[:, :, 1:] - flux_y[:, :, :-1]
    upward = 0.5 * (vertical_pad[:-1] + vertical_pad[1:])
    flux_z = vertical_scale * upward[None] * (0.5 * (field_lev[:, :-1] + field_lev[:, 1:]))
    div_z = flux_z[:, 1:] - flux_z[:, :-1]
    updated = field - (div_x + div_y) / center_cos[None, None, :, None] - div_z
    return (updated[0], updated[1], updated[2])


def solution(mesh):
    in_specs = (
        P("lev", "lat", None),
        P("lev", "lat", None),
        P("lev", "lat", None),
        P("lev", "lat", None),
        P(),
    )
    out_specs = (P("lev", "lat", None), P("lev", "lat", None), P("lev", "lat", None))
    return jax.shard_map(
        on_device, mesh=mesh, in_specs=in_specs, out_specs=out_specs, check_vma=False
    )
```

```python
import math

import jax
import numpy as np
import jax.numpy as jnp
from jax import lax
from jax.sharding import PartitionSpec as P

NLON = 2880
KMAX = 720
HALF = NLON // 2
CAP = 80

zonal_scale = 0.1
merid_scale = 0.1
vertical_scale = 0.1
mxu_precision = lax.Precision.HIGH


def shift(x, axis, up):
    size = lax.axis_size(axis)
    pairs = [(i, i + 1) for i in range(size - 1)]
    if not up:
        pairs = [(j, i) for i, j in pairs]
    return lax.ppermute(x, axis, pairs)


def group_shift(x, lat_group, up):
    lev_size = lax.axis_size("lev")
    pairs = []
    for lat in lat_group:
        for lev in range(lev_size - 1):
            source, target = lat * lev_size + lev, lat * lev_size + lev + 1
            pairs.append((source, target) if up else (target, source))
    return lax.ppermute(x, ("lat", "lev"), pairs)


def parity_table(parity):
    low = 48
    modes = np.arange(parity, KMAX, 2)
    k = np.concatenate([modes, modes])[None, :]
    is_sin = np.arange(KMAX)[None, :] >= KMAX // 2
    step = 2.0 * np.pi / NLON
    lo = (np.arange(low)[:, None] * k) % NLON * step
    hi = (low * np.arange(HALF // low)[:, None] * k) % NLON * step
    first = np.where(is_sin, np.sin(lo), np.cos(lo))
    turn = np.where(is_sin, np.cos(lo), -np.sin(lo))
    as_f32 = lambda v: jnp.asarray(v.astype(np.float32))
    table = (as_f32(first)[None] * as_f32(np.cos(hi))[:, None]
             + as_f32(turn)[None] * as_f32(np.sin(hi))[:, None])
    return table.reshape(HALF, KMAX)


def parity_weight(parity, cut):
    modes = np.arange(parity, KMAX, 2)
    mode_ids = jnp.asarray(np.concatenate([modes, modes]).astype(np.int32))
    factor = jnp.where(mode_ids == 0, jnp.float32(1.0), jnp.float32(2.0)) / NLON
    return jnp.where(mode_ids[None, :] <= cut[:, None], factor[None, :], jnp.float32(0.0))


def lowpass_rows(x, cut, tables):
    even_table, odd_table = tables
    first, second = x[:, :HALF], x[:, HALF:]
    spec_even = jnp.dot(first + second, even_table, precision=mxu_precision,
                        preferred_element_type=jnp.float32)
    spec_odd = jnp.dot(first - second, odd_table, precision=mxu_precision,
                       preferred_element_type=jnp.float32)
    dims = (((1,), (1,)), ((), ()))
    even_out = lax.dot_general(spec_even * parity_weight(0, cut), even_table, dims,
                               precision=mxu_precision, preferred_element_type=jnp.float32)
    odd_out = lax.dot_general(spec_odd * parity_weight(1, cut), odd_table, dims,
                              precision=mxu_precision, preferred_element_type=jnp.float32)
    summed = jnp.concatenate([even_out + odd_out, even_out - odd_out], axis=1)
    return jnp.where((cut < HALF)[:, None], summed, x)


def filtered(x, cut, tables):
    shape = x.shape
    rows = x.reshape(-1, NLON)
    cuts = jnp.broadcast_to(cut, shape[:-1]).reshape(-1)
    out = lax.cond(jnp.any(cut < HALF), lambda: lowpass_rows(rows, cuts, tables), lambda: rows)
    return out.reshape(shape)


def on_device(zonal_wind, merid_wind, tracer, vertical_wind, cutoff):
    lat_rows = zonal_wind.shape[1]
    lat_count = lax.axis_size("lat")
    lat_index = lax.axis_index("lat")
    total_rows = lat_rows * lat_count
    row_start = lat_index * lat_rows
    own_cut = lax.dynamic_slice_in_dim(cutoff, row_start, lat_rows)

    stacked = jnp.stack([zonal_wind, merid_wind, tracer])
    levels = stacked.shape[1]
    pole_rows = [min(j, total_rows - 1 - j) + 1 <= CAP for j in range(total_rows)]
    filter_lat = [i for i in range(lat_count) if any(pole_rows[i * lat_rows:(i + 1) * lat_rows])]
    plain_lat = [i for i in range(lat_count) if i not in filter_lat]
    top = jnp.concatenate([stacked[:, levels - 1], vertical_wind[levels - 1 :]], axis=0)
    bottom = jnp.concatenate([stacked[:, 0], vertical_wind[:1]], axis=0)
    below_plain = group_shift(top, plain_lat, True)
    above_plain = group_shift(bottom, plain_lat, False)

    tables = (parity_table(0), parity_table(1))
    stacked, below_plain, above_plain = lax.optimization_barrier((stacked, below_plain, above_plain))
    field = filtered(stacked, own_cut, tables)
    top = jnp.concatenate([field[:, levels - 1], vertical_wind[levels - 1 :]], axis=0)
    bottom = jnp.concatenate([field[:, 0], vertical_wind[:1]], axis=0)
    below_filtered = group_shift(top, filter_lat, True)
    above_filtered = group_shift(bottom, filter_lat, False)
    is_filter = jnp.any(lat_index == jnp.asarray(filter_lat, jnp.int32))
    below_all = jnp.where(is_filter, below_filtered, below_plain)
    above_all = jnp.where(is_filter, above_filtered, above_plain)
    below, below_wind = below_all[:3, None], below_all[3:]
    above, above_wind = above_all[:3, None], above_all[3:]
    south = shift(field[:, :, lat_rows - 1 :], "lat", True)
    north = shift(field[:, :, :1], "lat", False)

    vertical_pad = jnp.concatenate([below_wind, vertical_wind, above_wind], axis=0)
    field_lat = jnp.concatenate([south, field, north], axis=2)
    field_lev = jnp.concatenate([below, field, above], axis=1)

    face_ids = (row_start + jnp.arange(lat_rows + 1, dtype=jnp.int32)).astype(jnp.float32)
    face_cos = jnp.sin(face_ids * (math.pi / total_rows))
    center_ids = (row_start + jnp.arange(lat_rows, dtype=jnp.int32)).astype(jnp.float32)
    center_cos = jnp.sin((center_ids + 0.5) * (math.pi / total_rows))
    zonal_now = field[0]
    east_wind = 0.5 * (zonal_now + jnp.roll(zonal_now, -1, axis=2))
    flux_x = zonal_scale * east_wind[None] * (0.5 * (field + jnp.roll(field, -1, axis=3)))
    div_x = flux_x - jnp.roll(flux_x, 1, axis=3)
    merid_lat = field_lat[1]
    north_wind = 0.5 * (merid_lat[:, :-1] + merid_lat[:, 1:])
    flux_y = (
        merid_scale
        * face_cos[None, None, :, None]
        * north_wind[None]
        * (0.5 * (field_lat[:, :, :-1] + field_lat[:, :, 1:]))
    )
    div_y = flux_y[:, :, 1:] - flux_y[:, :, :-1]
    upward = 0.5 * (vertical_pad[:-1] + vertical_pad[1:])
    flux_z = vertical_scale * upward[None] * (0.5 * (field_lev[:, :-1] + field_lev[:, 1:]))
    div_z = flux_z[:, 1:] - flux_z[:, :-1]
    updated = field - (div_x + div_y) / center_cos[None, None, :, None] - div_z
    return (updated[0], updated[1], updated[2])


def solution(mesh):
    in_specs = (
        P("lev", "lat", None),
        P("lev", "lat", None),
        P("lev", "lat", None),
        P("lev", "lat", None),
        P(),
    )
    out_specs = (P("lev", "lat", None), P("lev", "lat", None), P("lev", "lat", None))
    return jax.shard_map(
        on_device, mesh=mesh, in_specs=in_specs, out_specs=out_specs, check_vma=False
    )
```

```python
import math

import jax
import numpy as np
import jax.numpy as jnp
from jax import lax
from jax.sharding import PartitionSpec as P

NLON = 2880
KMAX = 720
HALF = NLON // 2
CAP = 80

zonal_scale = 0.1
merid_scale = 0.1
vertical_scale = 0.1
mxu_precision = lax.Precision.HIGH


def shift(x, axis, up):
    size = lax.axis_size(axis)
    pairs = [(i, i + 1) for i in range(size - 1)]
    if not up:
        pairs = [(j, i) for i, j in pairs]
    return lax.ppermute(x, axis, pairs)


def group_shift(x, lat_group, up):
    lev_size = lax.axis_size("lev")
    pairs = []
    for lat in lat_group:
        for lev in range(lev_size - 1):
            source, target = lat * lev_size + lev, lat * lev_size + lev + 1
            pairs.append((source, target) if up else (target, source))
    return lax.ppermute(x, ("lat", "lev"), pairs)


def lat_group_shift(x, sources, up):
    lat_size, lev_size = lax.axis_size("lat"), lax.axis_size("lev")
    step = 1 if up else -1
    pairs = [(lat * lev_size + lev, (lat + step) * lev_size + lev)
             for lat in sources if 0 <= lat + step < lat_size for lev in range(lev_size)]
    return lax.ppermute(x, ("lat", "lev"), pairs)


def parity_table(parity):
    low = 48
    modes = np.arange(parity, KMAX, 2)
    k = np.concatenate([modes, modes])[None, :]
    is_sin = np.arange(KMAX)[None, :] >= KMAX // 2
    step = 2.0 * np.pi / NLON
    lo = (np.arange(low)[:, None] * k) % NLON * step
    hi = (low * np.arange(HALF // low)[:, None] * k) % NLON * step
    first = np.where(is_sin, np.sin(lo), np.cos(lo))
    turn = np.where(is_sin, np.cos(lo), -np.sin(lo))
    as_f32 = lambda v: jnp.asarray(v.astype(np.float32))
    table = (as_f32(first)[None] * as_f32(np.cos(hi))[:, None]
             + as_f32(turn)[None] * as_f32(np.sin(hi))[:, None])
    return table.reshape(HALF, KMAX)


def parity_weight(parity, cut):
    modes = np.arange(parity, KMAX, 2)
    mode_ids = jnp.asarray(np.concatenate([modes, modes]).astype(np.int32))
    factor = jnp.where(mode_ids == 0, jnp.float32(1.0), jnp.float32(2.0)) / NLON
    return jnp.where(mode_ids[None, :] <= cut[:, None], factor[None, :], jnp.float32(0.0))


def lowpass_rows(x, cut, tables):
    even_table, odd_table = tables
    first, second = x[:, :HALF], x[:, HALF:]
    spec_even = jnp.dot(first + second, even_table, precision=mxu_precision,
                        preferred_element_type=jnp.float32)
    spec_odd = jnp.dot(first - second, odd_table, precision=mxu_precision,
                       preferred_element_type=jnp.float32)
    dims = (((1,), (1,)), ((), ()))
    even_out = lax.dot_general(spec_even * parity_weight(0, cut), even_table, dims,
                               precision=mxu_precision, preferred_element_type=jnp.float32)
    odd_out = lax.dot_general(spec_odd * parity_weight(1, cut), odd_table, dims,
                              precision=mxu_precision, preferred_element_type=jnp.float32)
    summed = jnp.concatenate([even_out + odd_out, even_out - odd_out], axis=1)
    return jnp.where((cut < HALF)[:, None], summed, x)


def filtered(x, cut, tables):
    shape = x.shape
    rows = x.reshape(-1, NLON)
    cuts = jnp.broadcast_to(cut, shape[:-1]).reshape(-1)
    out = lax.cond(jnp.any(cut < HALF), lambda: lowpass_rows(rows, cuts, tables), lambda: rows)
    return out.reshape(shape)


def on_device(zonal_wind, merid_wind, tracer, vertical_wind, cutoff):
    lat_rows = zonal_wind.shape[1]
    lat_count = lax.axis_size("lat")
    lat_index = lax.axis_index("lat")
    total_rows = lat_rows * lat_count
    row_start = lat_index * lat_rows
    own_cut = lax.dynamic_slice_in_dim(cutoff, row_start, lat_rows)

    stacked = jnp.stack([zonal_wind, merid_wind, tracer])
    levels = stacked.shape[1]
    pole_rows = [min(j, total_rows - 1 - j) + 1 <= CAP for j in range(total_rows)]
    filter_lat = [i for i in range(lat_count) if any(pole_rows[i * lat_rows:(i + 1) * lat_rows])]
    plain_lat = [i for i in range(lat_count) if i not in filter_lat]
    top = jnp.concatenate([stacked[:, levels - 1], vertical_wind[levels - 1 :]], axis=0)
    bottom = jnp.concatenate([stacked[:, 0], vertical_wind[:1]], axis=0)
    below_plain = group_shift(top, plain_lat, True)
    above_plain = group_shift(bottom, plain_lat, False)

    tables = (parity_table(0), parity_table(1))
    south_plain = lat_group_shift(stacked[:, :, lat_rows - 1 :], plain_lat, True)
    north_plain = lat_group_shift(stacked[:, :, :1], plain_lat, False)
    stacked, below_plain, above_plain, south_plain, north_plain = lax.optimization_barrier(
        (stacked, below_plain, above_plain, south_plain, north_plain))
    field = filtered(stacked, own_cut, tables)
    top = jnp.concatenate([field[:, levels - 1], vertical_wind[levels - 1 :]], axis=0)
    bottom = jnp.concatenate([field[:, 0], vertical_wind[:1]], axis=0)
    below_filtered = group_shift(top, filter_lat, True)
    above_filtered = group_shift(bottom, filter_lat, False)
    is_filter = jnp.any(lat_index == jnp.asarray(filter_lat, jnp.int32))
    below_all = jnp.where(is_filter, below_filtered, below_plain)
    above_all = jnp.where(is_filter, above_filtered, above_plain)
    below, below_wind = below_all[:3, None], below_all[3:]
    above, above_wind = above_all[:3, None], above_all[3:]
    south_filtered = lat_group_shift(field[:, :, lat_rows - 1 :], filter_lat, True)
    north_filtered = lat_group_shift(field[:, :, :1], filter_lat, False)
    south_is_filter = jnp.any(lat_index - 1 == jnp.asarray(filter_lat, jnp.int32))
    north_is_filter = jnp.any(lat_index + 1 == jnp.asarray(filter_lat, jnp.int32))
    south = jnp.where(south_is_filter, south_filtered, south_plain)
    north = jnp.where(north_is_filter, north_filtered, north_plain)

    vertical_pad = jnp.concatenate([below_wind, vertical_wind, above_wind], axis=0)
    field_lat = jnp.concatenate([south, field, north], axis=2)
    field_lev = jnp.concatenate([below, field, above], axis=1)

    face_ids = (row_start + jnp.arange(lat_rows + 1, dtype=jnp.int32)).astype(jnp.float32)
    face_cos = jnp.sin(face_ids * (math.pi / total_rows))
    center_ids = (row_start + jnp.arange(lat_rows, dtype=jnp.int32)).astype(jnp.float32)
    center_cos = jnp.sin((center_ids + 0.5) * (math.pi / total_rows))
    zonal_now = field[0]
    east_wind = 0.5 * (zonal_now + jnp.roll(zonal_now, -1, axis=2))
    flux_x = zonal_scale * east_wind[None] * (0.5 * (field + jnp.roll(field, -1, axis=3)))
    div_x = flux_x - jnp.roll(flux_x, 1, axis=3)
    merid_lat = field_lat[1]
    north_wind = 0.5 * (merid_lat[:, :-1] + merid_lat[:, 1:])
    flux_y = (
        merid_scale
        * face_cos[None, None, :, None]
        * north_wind[None]
        * (0.5 * (field_lat[:, :, :-1] + field_lat[:, :, 1:]))
    )
    div_y = flux_y[:, :, 1:] - flux_y[:, :, :-1]
    upward = 0.5 * (vertical_pad[:-1] + vertical_pad[1:])
    flux_z = vertical_scale * upward[None] * (0.5 * (field_lev[:, :-1] + field_lev[:, 1:]))
    div_z = flux_z[:, 1:] - flux_z[:, :-1]
    updated = field - (div_x + div_y) / center_cos[None, None, :, None] - div_z
    return (updated[0], updated[1], updated[2])


def solution(mesh):
    in_specs = (
        P("lev", "lat", None),
        P("lev", "lat", None),
        P("lev", "lat", None),
        P("lev", "lat", None),
        P(),
    )
    out_specs = (P("lev", "lat", None), P("lev", "lat", None), P("lev", "lat", None))
    return jax.shard_map(
        on_device, mesh=mesh, in_specs=in_specs, out_specs=out_specs, check_vma=False
    )
```

```python
import math

import jax
import numpy as np
import jax.numpy as jnp
from jax import lax
from jax.sharding import PartitionSpec as P

NLON = 2880
KMAX = 720
HALF = NLON // 2
CAP = 80

zonal_scale = 0.1
merid_scale = 0.1
vertical_scale = 0.1
mxu_precision = lax.Precision.HIGH


def shift(x, axis, up):
    size = lax.axis_size(axis)
    pairs = [(i, i + 1) for i in range(size - 1)]
    if not up:
        pairs = [(j, i) for i, j in pairs]
    return lax.ppermute(x, axis, pairs)


def group_shift(x, lat_group, up):
    lev_size = lax.axis_size("lev")
    pairs = []
    for lat in lat_group:
        for lev in range(lev_size - 1):
            source, target = lat * lev_size + lev, lat * lev_size + lev + 1
            pairs.append((source, target) if up else (target, source))
    return lax.ppermute(x, ("lat", "lev"), pairs)


def lat_group_shift(x, group, up):
    lev_size = lax.axis_size("lev")
    step = 1 if up else -1
    pairs = [(lat * lev_size + lev, (lat + step) * lev_size + lev)
             for lat in group if lat + step in group for lev in range(lev_size)]
    return lax.ppermute(x, ("lat", "lev"), pairs)


def parity_table(parity):
    low = 48
    modes = np.arange(parity, KMAX, 2)
    k = np.concatenate([modes, modes])[None, :]
    is_sin = np.arange(KMAX)[None, :] >= KMAX // 2
    step = 2.0 * np.pi / NLON
    lo = (np.arange(low)[:, None] * k) % NLON * step
    hi = (low * np.arange(HALF // low)[:, None] * k) % NLON * step
    first = np.where(is_sin, np.sin(lo), np.cos(lo))
    turn = np.where(is_sin, np.cos(lo), -np.sin(lo))
    as_f32 = lambda v: jnp.asarray(v.astype(np.float32))
    table = (as_f32(first)[None] * as_f32(np.cos(hi))[:, None]
             + as_f32(turn)[None] * as_f32(np.sin(hi))[:, None])
    return table.reshape(HALF, KMAX)


def parity_weight(parity, cut):
    modes = np.arange(parity, KMAX, 2)
    mode_ids = jnp.asarray(np.concatenate([modes, modes]).astype(np.int32))
    factor = jnp.where(mode_ids == 0, jnp.float32(1.0), jnp.float32(2.0)) / NLON
    return jnp.where(mode_ids[None, :] <= cut[:, None], factor[None, :], jnp.float32(0.0))


def lowpass_rows(x, cut, tables):
    even_table, odd_table = tables
    first, second = x[:, :HALF], x[:, HALF:]
    spec_even = jnp.dot(first + second, even_table, precision=mxu_precision,
                        preferred_element_type=jnp.float32)
    spec_odd = jnp.dot(first - second, odd_table, precision=mxu_precision,
                       preferred_element_type=jnp.float32)
    dims = (((1,), (1,)), ((), ()))
    even_out = lax.dot_general(spec_even * parity_weight(0, cut), even_table, dims,
                               precision=mxu_precision, preferred_element_type=jnp.float32)
    odd_out = lax.dot_general(spec_odd * parity_weight(1, cut), odd_table, dims,
                              precision=mxu_precision, preferred_element_type=jnp.float32)
    summed = jnp.concatenate([even_out + odd_out, even_out - odd_out], axis=1)
    return jnp.where((cut < HALF)[:, None], summed, x)


def filtered(x, cut, tables):
    shape = x.shape
    rows = x.reshape(-1, NLON)
    cuts = jnp.broadcast_to(cut, shape[:-1]).reshape(-1)
    out = lax.cond(jnp.any(cut < HALF), lambda: lowpass_rows(rows, cuts, tables), lambda: rows)
    return out.reshape(shape)


def on_device(zonal_wind, merid_wind, tracer, vertical_wind, cutoff):
    lat_rows = zonal_wind.shape[1]
    lat_count = lax.axis_size("lat")
    lat_index = lax.axis_index("lat")
    total_rows = lat_rows * lat_count
    row_start = lat_index * lat_rows
    own_cut = lax.dynamic_slice_in_dim(cutoff, row_start, lat_rows)

    stacked = jnp.stack([zonal_wind, merid_wind, tracer])
    levels = stacked.shape[1]
    pole_rows = [min(j, total_rows - 1 - j) + 1 <= CAP for j in range(total_rows)]
    filter_lat = [i for i in range(lat_count) if any(pole_rows[i * lat_rows:(i + 1) * lat_rows])]
    plain_lat = [i for i in range(lat_count) if i not in filter_lat]
    top = jnp.concatenate([stacked[:, levels - 1], vertical_wind[levels - 1 :]], axis=0)
    bottom = jnp.concatenate([stacked[:, 0], vertical_wind[:1]], axis=0)
    below_plain = group_shift(top, plain_lat, True)
    above_plain = group_shift(bottom, plain_lat, False)

    tables = (parity_table(0), parity_table(1))
    south_plain = shift(stacked[:, :, lat_rows - 1 :], "lat", True)
    north_plain = shift(stacked[:, :, :1], "lat", False)
    stacked, south_plain, north_plain = lax.optimization_barrier((stacked, south_plain, north_plain))
    field = filtered(stacked, own_cut, tables)
    top = jnp.concatenate([field[:, levels - 1], vertical_wind[levels - 1 :]], axis=0)
    bottom = jnp.concatenate([field[:, 0], vertical_wind[:1]], axis=0)
    below_filtered = group_shift(top, filter_lat, True)
    above_filtered = group_shift(bottom, filter_lat, False)
    is_filter = jnp.any(lat_index == jnp.asarray(filter_lat, jnp.int32))
    below_all = jnp.where(is_filter, below_filtered, below_plain)
    above_all = jnp.where(is_filter, above_filtered, above_plain)
    below, below_wind = below_all[:3, None], below_all[3:]
    above, above_wind = above_all[:3, None], above_all[3:]
    south_filtered = lat_group_shift(field[:, :, lat_rows - 1 :], filter_lat, True)
    north_filtered = lat_group_shift(field[:, :, :1], filter_lat, False)
    south_is_filter = jnp.any(lat_index - 1 == jnp.asarray(filter_lat, jnp.int32))
    north_is_filter = jnp.any(lat_index + 1 == jnp.asarray(filter_lat, jnp.int32))
    halo_ids = jnp.stack([row_start - 1, row_start + lat_rows])
    halo_cut = cutoff[jnp.clip(halo_ids, 0, total_rows - 1)]
    halo_raw = jnp.concatenate([south_plain, north_plain], axis=2)
    halo_rows = halo_raw.reshape(-1, NLON)
    halo_cuts = jnp.broadcast_to(halo_cut, halo_raw.shape[:-1]).reshape(-1)
    halo_own = lax.cond(jnp.logical_and(jnp.logical_not(is_filter), jnp.any(halo_cut < HALF)),
                        lambda: lowpass_rows(halo_rows, halo_cuts, tables), lambda: halo_rows)
    halo_own = halo_own.reshape(halo_raw.shape)
    south = jnp.where(jnp.logical_and(is_filter, south_is_filter), south_filtered, halo_own[:, :, :1])
    north = jnp.where(jnp.logical_and(is_filter, north_is_filter), north_filtered, halo_own[:, :, 1:])

    vertical_pad = jnp.concatenate([below_wind, vertical_wind, above_wind], axis=0)
    field_lat = jnp.concatenate([south, field, north], axis=2)
    field_lev = jnp.concatenate([below, field, above], axis=1)

    face_ids = (row_start + jnp.arange(lat_rows + 1, dtype=jnp.int32)).astype(jnp.float32)
    face_cos = jnp.sin(face_ids * (math.pi / total_rows))
    center_ids = (row_start + jnp.arange(lat_rows, dtype=jnp.int32)).astype(jnp.float32)
    center_cos = jnp.sin((center_ids + 0.5) * (math.pi / total_rows))
    zonal_now = field[0]
    east_wind = 0.5 * (zonal_now + jnp.roll(zonal_now, -1, axis=2))
    flux_x = zonal_scale * east_wind[None] * (0.5 * (field + jnp.roll(field, -1, axis=3)))
    div_x = flux_x - jnp.roll(flux_x, 1, axis=3)
    merid_lat = field_lat[1]
    north_wind = 0.5 * (merid_lat[:, :-1] + merid_lat[:, 1:])
    flux_y = (
        merid_scale
        * face_cos[None, None, :, None]
        * north_wind[None]
        * (0.5 * (field_lat[:, :, :-1] + field_lat[:, :, 1:]))
    )
    div_y = flux_y[:, :, 1:] - flux_y[:, :, :-1]
    upward = 0.5 * (vertical_pad[:-1] + vertical_pad[1:])
    flux_z = vertical_scale * upward[None] * (0.5 * (field_lev[:, :-1] + field_lev[:, 1:]))
    div_z = flux_z[:, 1:] - flux_z[:, :-1]
    updated = field - (div_x + div_y) / center_cos[None, None, :, None] - div_z
    return (updated[0], updated[1], updated[2])


def solution(mesh):
    in_specs = (
        P("lev", "lat", None),
        P("lev", "lat", None),
        P("lev", "lat", None),
        P("lev", "lat", None),
        P(),
    )
    out_specs = (P("lev", "lat", None), P("lev", "lat", None), P("lev", "lat", None))
    return jax.shard_map(
        on_device, mesh=mesh, in_specs=in_specs, out_specs=out_specs, check_vma=False
    )
```

```python
import math

import jax
import numpy as np
import jax.numpy as jnp
from jax import lax
from jax.sharding import PartitionSpec as P

NLON = 2880
KMAX = 720
HALF = NLON // 2
CAP = 80

zonal_scale = 0.1
merid_scale = 0.1
vertical_scale = 0.1
mxu_precision = lax.Precision.HIGH


def shift(x, axis, up):
    size = lax.axis_size(axis)
    pairs = [(i, i + 1) for i in range(size - 1)]
    if not up:
        pairs = [(j, i) for i, j in pairs]
    return lax.ppermute(x, axis, pairs)


def group_shift(x, lat_group, up):
    lev_size = lax.axis_size("lev")
    pairs = []
    for lat in lat_group:
        for lev in range(lev_size - 1):
            source, target = lat * lev_size + lev, lat * lev_size + lev + 1
            pairs.append((source, target) if up else (target, source))
    return lax.ppermute(x, ("lat", "lev"), pairs)


def lat_group_shift(x, group, up):
    lev_size = lax.axis_size("lev")
    step = 1 if up else -1
    pairs = [(lat * lev_size + lev, (lat + step) * lev_size + lev)
             for lat in group if lat + step in group for lev in range(lev_size)]
    return lax.ppermute(x, ("lat", "lev"), pairs)


def parity_table(parity, low=48):
    modes = np.arange(parity, KMAX, 2)
    k = np.concatenate([modes, modes])[None, :]
    is_sin = np.arange(KMAX)[None, :] >= KMAX // 2
    step = 2.0 * np.pi / NLON
    lo = (np.arange(low)[:, None] * k) % NLON * step
    hi = (low * np.arange(HALF // low)[:, None] * k) % NLON * step
    first = np.where(is_sin, np.sin(lo), np.cos(lo))
    turn = np.where(is_sin, np.cos(lo), -np.sin(lo))
    as_f32 = lambda v: jnp.asarray(v.astype(np.float32))
    table = (as_f32(first)[None] * as_f32(np.cos(hi))[:, None]
             + as_f32(turn)[None] * as_f32(np.sin(hi))[:, None])
    return table.reshape(HALF, KMAX)


def parity_weight(parity, cut):
    modes = np.arange(parity, KMAX, 2)
    mode_ids = jnp.asarray(np.concatenate([modes, modes]).astype(np.int32))
    factor = jnp.where(mode_ids == 0, jnp.float32(1.0), jnp.float32(2.0)) / NLON
    return jnp.where(mode_ids[None, :] <= cut[:, None], factor[None, :], jnp.float32(0.0))


def lowpass_rows(x, cut, tables):
    even_table, odd_table = tables
    first, second = x[:, :HALF], x[:, HALF:]
    spec_even = jnp.dot(first + second, even_table, precision=mxu_precision,
                        preferred_element_type=jnp.float32)
    spec_odd = jnp.dot(first - second, odd_table, precision=mxu_precision,
                       preferred_element_type=jnp.float32)
    dims = (((1,), (1,)), ((), ()))
    even_out = lax.dot_general(spec_even * parity_weight(0, cut), even_table, dims,
                               precision=mxu_precision, preferred_element_type=jnp.float32)
    odd_out = lax.dot_general(spec_odd * parity_weight(1, cut), odd_table, dims,
                              precision=mxu_precision, preferred_element_type=jnp.float32)
    summed = jnp.concatenate([even_out + odd_out, even_out - odd_out], axis=1)
    return jnp.where((cut < HALF)[:, None], summed, x)


def filtered(x, cut, run=None, low=48):
    shape = x.shape
    rows = x.reshape(-1, NLON)
    cuts = jnp.broadcast_to(cut, shape[:-1]).reshape(-1)
    run = jnp.any(cut < HALF) if run is None else run
    out = lax.cond(run, lambda: lowpass_rows(rows, cuts, (parity_table(0, low), parity_table(1, low))), lambda: rows)
    return out.reshape(shape)


def on_device(zonal_wind, merid_wind, tracer, vertical_wind, cutoff):
    lat_rows = zonal_wind.shape[1]
    lat_count = lax.axis_size("lat")
    lat_index = lax.axis_index("lat")
    total_rows = lat_rows * lat_count
    row_start = lat_index * lat_rows
    own_cut = lax.dynamic_slice_in_dim(cutoff, row_start, lat_rows)

    stacked = jnp.stack([zonal_wind, merid_wind, tracer])
    levels = stacked.shape[1]
    pole_rows = [min(j, total_rows - 1 - j) + 1 <= CAP for j in range(total_rows)]
    filter_lat = [i for i in range(lat_count) if any(pole_rows[i * lat_rows:(i + 1) * lat_rows])]
    plain_lat = [i for i in range(lat_count) if i not in filter_lat]
    top = jnp.concatenate([stacked[:, levels - 1], vertical_wind[levels - 1 :]], axis=0)
    bottom = jnp.concatenate([stacked[:, 0], vertical_wind[:1]], axis=0)
    below_plain = group_shift(top, plain_lat, True)
    above_plain = group_shift(bottom, plain_lat, False)

    south_raw = shift(stacked[:, :, lat_rows - 1 :], "lat", True)
    north_raw = shift(stacked[:, :, :1], "lat", False)
    is_filter = jnp.any(lat_index == jnp.asarray(filter_lat, jnp.int32))
    halo_ids = jnp.stack([row_start - 1, row_start + lat_rows])
    halo_cut = cutoff[jnp.clip(halo_ids, 0, total_rows - 1)]
    halo_own = filtered(jnp.concatenate([south_raw, north_raw], axis=2), halo_cut,
                        jnp.logical_and(jnp.logical_not(is_filter), jnp.any(halo_cut < HALF)), 40)
    stacked, below_plain, above_plain, halo_own = lax.optimization_barrier(
        (stacked, below_plain, above_plain, halo_own))
    field = filtered(stacked, own_cut)
    top = jnp.concatenate([field[:, levels - 1], vertical_wind[levels - 1 :]], axis=0)
    bottom = jnp.concatenate([field[:, 0], vertical_wind[:1]], axis=0)
    below_filtered = group_shift(top, filter_lat, True)
    above_filtered = group_shift(bottom, filter_lat, False)
    below_all = jnp.where(is_filter, below_filtered, below_plain)
    above_all = jnp.where(is_filter, above_filtered, above_plain)
    below, below_wind = below_all[:3, None], below_all[3:]
    above, above_wind = above_all[:3, None], above_all[3:]
    south_filtered = lat_group_shift(field[:, :, lat_rows - 1 :], filter_lat, True)
    north_filtered = lat_group_shift(field[:, :, :1], filter_lat, False)
    south_is_filter = jnp.any(lat_index - 1 == jnp.asarray(filter_lat, jnp.int32))
    north_is_filter = jnp.any(lat_index + 1 == jnp.asarray(filter_lat, jnp.int32))
    south = jnp.where(jnp.logical_and(is_filter, south_is_filter), south_filtered, halo_own[:, :, :1])
    north = jnp.where(jnp.logical_and(is_filter, north_is_filter), north_filtered, halo_own[:, :, 1:])

    vertical_pad = jnp.concatenate([below_wind, vertical_wind, above_wind], axis=0)
    field_lat = jnp.concatenate([south, field, north], axis=2)
    field_lev = jnp.concatenate([below, field, above], axis=1)

    face_ids = (row_start + jnp.arange(lat_rows + 1, dtype=jnp.int32)).astype(jnp.float32)
    face_cos = jnp.sin(face_ids * (math.pi / total_rows))
    center_ids = (row_start + jnp.arange(lat_rows, dtype=jnp.int32)).astype(jnp.float32)
    center_cos = jnp.sin((center_ids + 0.5) * (math.pi / total_rows))
    zonal_now = field[0]
    east_wind = 0.5 * (zonal_now + jnp.roll(zonal_now, -1, axis=2))
    flux_x = zonal_scale * east_wind[None] * (0.5 * (field + jnp.roll(field, -1, axis=3)))
    div_x = flux_x - jnp.roll(flux_x, 1, axis=3)
    merid_lat = field_lat[1]
    north_wind = 0.5 * (merid_lat[:, :-1] + merid_lat[:, 1:])
    flux_y = (
        merid_scale
        * face_cos[None, None, :, None]
        * north_wind[None]
        * (0.5 * (field_lat[:, :, :-1] + field_lat[:, :, 1:]))
    )
    div_y = flux_y[:, :, 1:] - flux_y[:, :, :-1]
    upward = 0.5 * (vertical_pad[:-1] + vertical_pad[1:])
    flux_z = vertical_scale * upward[None] * (0.5 * (field_lev[:, :-1] + field_lev[:, 1:]))
    div_z = flux_z[:, 1:] - flux_z[:, :-1]
    updated = field - (div_x + div_y) / center_cos[None, None, :, None] - div_z
    return (updated[0], updated[1], updated[2])


def solution(mesh):
    in_specs = (
        P("lev", "lat", None),
        P("lev", "lat", None),
        P("lev", "lat", None),
        P("lev", "lat", None),
        P(),
    )
    out_specs = (P("lev", "lat", None), P("lev", "lat", None), P("lev", "lat", None))
    return jax.shard_map(
        on_device, mesh=mesh, in_specs=in_specs, out_specs=out_specs, check_vma=False
    )
```

```python
import math

import jax
import numpy as np
import jax.numpy as jnp
from jax import lax
from jax.sharding import PartitionSpec as P

NLON = 2880
KMAX = 720
HALF = NLON // 2
CAP = 80

zonal_scale = 0.1
merid_scale = 0.1
vertical_scale = 0.1
mxu_precision = lax.Precision.HIGH


def shift(x, axis, up):
    size = lax.axis_size(axis)
    pairs = [(i, i + 1) for i in range(size - 1)]
    if not up:
        pairs = [(j, i) for i, j in pairs]
    return lax.ppermute(x, axis, pairs)


def group_shift(x, lat_group, up):
    lev_size = lax.axis_size("lev")
    pairs = []
    for lat in lat_group:
        for lev in range(lev_size - 1):
            source, target = lat * lev_size + lev, lat * lev_size + lev + 1
            pairs.append((source, target) if up else (target, source))
    return lax.ppermute(x, ("lat", "lev"), pairs)


def lat_group_shift(x, sources, up):
    lat_size, lev_size = lax.axis_size("lat"), lax.axis_size("lev")
    step = 1 if up else -1
    pairs = [(lat * lev_size + lev, (lat + step) * lev_size + lev)
             for lat in sources if 0 <= lat + step < lat_size for lev in range(lev_size)]
    return lax.ppermute(x, ("lat", "lev"), pairs)


def parity_table(parity):
    low = 48
    modes = np.arange(parity, KMAX, 2)
    k = np.concatenate([modes, modes])[None, :]
    is_sin = np.arange(KMAX)[None, :] >= KMAX // 2
    step = 2.0 * np.pi / NLON
    lo = (np.arange(low)[:, None] * k) % NLON * step
    hi = (low * np.arange(HALF // low)[:, None] * k) % NLON * step
    first = np.where(is_sin, np.sin(lo), np.cos(lo))
    turn = np.where(is_sin, np.cos(lo), -np.sin(lo))
    as_f32 = lambda v: jnp.asarray(v.astype(np.float32))
    table = (as_f32(first)[None] * as_f32(np.cos(hi))[:, None]
             + as_f32(turn)[None] * as_f32(np.sin(hi))[:, None])
    return table.reshape(HALF, KMAX)


def parity_weight(parity, cut):
    modes = np.arange(parity, KMAX, 2)
    mode_ids = jnp.asarray(np.concatenate([modes, modes]).astype(np.int32))
    factor = jnp.where(mode_ids == 0, jnp.float32(1.0), jnp.float32(2.0)) / NLON
    return jnp.where(mode_ids[None, :] <= cut[:, None], factor[None, :], jnp.float32(0.0))


def lowpass_rows(x, cut, tables):
    even_table, odd_table = tables
    first, second = x[:, :HALF], x[:, HALF:]
    spec_even = jnp.dot(first + second, even_table, precision=mxu_precision,
                        preferred_element_type=jnp.float32)
    spec_odd = jnp.dot(first - second, odd_table, precision=mxu_precision,
                       preferred_element_type=jnp.float32)
    dims = (((1,), (1,)), ((), ()))
    even_out = lax.dot_general(spec_even * parity_weight(0, cut), even_table, dims,
                               precision=mxu_precision, preferred_element_type=jnp.float32)
    odd_out = lax.dot_general(spec_odd * parity_weight(1, cut), odd_table, dims,
                              precision=mxu_precision, preferred_element_type=jnp.float32)
    summed = jnp.concatenate([even_out + odd_out, even_out - odd_out], axis=1)
    return jnp.where((cut < HALF)[:, None], summed, x)


def filtered(x, cut, tables):
    shape = x.shape
    rows = x.reshape(-1, NLON)
    cuts = jnp.broadcast_to(cut, shape[:-1]).reshape(-1)
    out = lax.cond(jnp.any(cut < HALF), lambda: lowpass_rows(rows, cuts, tables), lambda: rows)
    return out.reshape(shape)


def on_device(zonal_wind, merid_wind, tracer, vertical_wind, cutoff):
    lat_rows = zonal_wind.shape[1]
    lat_count = lax.axis_size("lat")
    lat_index = lax.axis_index("lat")
    total_rows = lat_rows * lat_count
    row_start = lat_index * lat_rows
    own_cut = lax.dynamic_slice_in_dim(cutoff, row_start, lat_rows)

    stacked = jnp.stack([zonal_wind, merid_wind, tracer])
    levels = stacked.shape[1]
    pole_rows = [min(j, total_rows - 1 - j) + 1 <= CAP for j in range(total_rows)]
    filter_lat = [i for i in range(lat_count) if any(pole_rows[i * lat_rows:(i + 1) * lat_rows])]
    plain_lat = [i for i in range(lat_count) if i not in filter_lat]
    top = jnp.concatenate([stacked[:, levels - 1], vertical_wind[levels - 1 :]], axis=0)
    bottom = jnp.concatenate([stacked[:, 0], vertical_wind[:1]], axis=0)
    below_plain = group_shift(top, plain_lat, True)
    above_plain = group_shift(bottom, plain_lat, False)

    tables = (parity_table(0), parity_table(1))
    south_plain = lat_group_shift(stacked[:, :, lat_rows - 1 :], plain_lat, True)
    north_plain = lat_group_shift(stacked[:, :, :1], plain_lat, False)
    stacked, below_plain, above_plain, south_plain, north_plain = lax.optimization_barrier(
        (stacked, below_plain, above_plain, south_plain, north_plain))
    field = filtered(stacked, own_cut, tables)
    top = jnp.concatenate([field[:, levels - 1], vertical_wind[levels - 1 :]], axis=0)
    bottom = jnp.concatenate([field[:, 0], vertical_wind[:1]], axis=0)
    below_filtered = group_shift(top, filter_lat, True)
    above_filtered = group_shift(bottom, filter_lat, False)
    is_filter = jnp.any(lat_index == jnp.asarray(filter_lat, jnp.int32))
    below_all = jnp.where(is_filter, below_filtered, below_plain)
    above_all = jnp.where(is_filter, above_filtered, above_plain)
    below, below_wind = below_all[:3, None], below_all[3:]
    above, above_wind = above_all[:3, None], above_all[3:]
    south_source, north_source, _ = lax.optimization_barrier(
        (field[:, :, lat_rows - 1 :], field[:, :, :1], (below_filtered, above_filtered)))
    south_filtered = lat_group_shift(south_source, filter_lat, True)
    north_filtered = lat_group_shift(north_source, filter_lat, False)
    south_is_filter = jnp.any(lat_index - 1 == jnp.asarray(filter_lat, jnp.int32))
    north_is_filter = jnp.any(lat_index + 1 == jnp.asarray(filter_lat, jnp.int32))
    south = jnp.where(south_is_filter, south_filtered, south_plain)
    north = jnp.where(north_is_filter, north_filtered, north_plain)

    vertical_pad = jnp.concatenate([below_wind, vertical_wind, above_wind], axis=0)
    field_lat = jnp.concatenate([south, field, north], axis=2)
    field_lev = jnp.concatenate([below, field, above], axis=1)

    face_ids = (row_start + jnp.arange(lat_rows + 1, dtype=jnp.int32)).astype(jnp.float32)
    face_cos = jnp.sin(face_ids * (math.pi / total_rows))
    center_ids = (row_start + jnp.arange(lat_rows, dtype=jnp.int32)).astype(jnp.float32)
    center_cos = jnp.sin((center_ids + 0.5) * (math.pi / total_rows))
    zonal_now = field[0]
    east_wind = 0.5 * (zonal_now + jnp.roll(zonal_now, -1, axis=2))
    flux_x = zonal_scale * east_wind[None] * (0.5 * (field + jnp.roll(field, -1, axis=3)))
    div_x = flux_x - jnp.roll(flux_x, 1, axis=3)
    merid_lat = field_lat[1]
    north_wind = 0.5 * (merid_lat[:, :-1] + merid_lat[:, 1:])
    flux_y = (
        merid_scale
        * face_cos[None, None, :, None]
        * north_wind[None]
        * (0.5 * (field_lat[:, :, :-1] + field_lat[:, :, 1:]))
    )
    div_y = flux_y[:, :, 1:] - flux_y[:, :, :-1]
    upward = 0.5 * (vertical_pad[:-1] + vertical_pad[1:])
    flux_z = vertical_scale * upward[None] * (0.5 * (field_lev[:, :-1] + field_lev[:, 1:]))
    div_z = flux_z[:, 1:] - flux_z[:, :-1]
    updated = field - (div_x + div_y) / center_cos[None, None, :, None] - div_z
    return (updated[0], updated[1], updated[2])


def solution(mesh):
    in_specs = (
        P("lev", "lat", None),
        P("lev", "lat", None),
        P("lev", "lat", None),
        P("lev", "lat", None),
        P(),
    )
    out_specs = (P("lev", "lat", None), P("lev", "lat", None), P("lev", "lat", None))
    return jax.shard_map(
        on_device, mesh=mesh, in_specs=in_specs, out_specs=out_specs, check_vma=False
    )
```

```python
import math

import jax
import numpy as np
import jax.numpy as jnp
from jax import lax
from jax.sharding import PartitionSpec as P

NLON = 2880
KMAX = 720
HALF = NLON // 2
CAP = 80

zonal_scale = 0.1
merid_scale = 0.1
vertical_scale = 0.1
mxu_precision = lax.Precision.HIGH


def shift(x, axis, up):
    size = lax.axis_size(axis)
    pairs = [(i, i + 1) for i in range(size - 1)]
    if not up:
        pairs = [(j, i) for i, j in pairs]
    return lax.ppermute(x, axis, pairs)


def group_shift(x, lat_group, up):
    lev_size = lax.axis_size("lev")
    pairs = []
    for lat in lat_group:
        for lev in range(lev_size - 1):
            source, target = lat * lev_size + lev, lat * lev_size + lev + 1
            pairs.append((source, target) if up else (target, source))
    return lax.ppermute(x, ("lat", "lev"), pairs)


def lat_group_shift(x, sources, up):
    lat_size, lev_size = lax.axis_size("lat"), lax.axis_size("lev")
    step = 1 if up else -1
    pairs = [(lat * lev_size + lev, (lat + step) * lev_size + lev)
             for lat in sources if 0 <= lat + step < lat_size for lev in range(lev_size)]
    return lax.ppermute(x, ("lat", "lev"), pairs)


def parity_table(parity):
    low = 48
    modes = np.arange(parity, KMAX, 2)
    k = np.concatenate([modes, modes])[None, :]
    is_sin = np.arange(KMAX)[None, :] >= KMAX // 2
    step = 2.0 * np.pi / NLON
    lo = (np.arange(low)[:, None] * k) % NLON * step
    hi = (low * np.arange(HALF // low)[:, None] * k) % NLON * step
    first = np.where(is_sin, np.sin(lo), np.cos(lo))
    turn = np.where(is_sin, np.cos(lo), -np.sin(lo))
    as_f32 = lambda v: jnp.asarray(v.astype(np.float32))
    table = (as_f32(first)[None] * as_f32(np.cos(hi))[:, None]
             + as_f32(turn)[None] * as_f32(np.sin(hi))[:, None])
    return table.reshape(HALF, KMAX)


def parity_weight(parity, cut):
    modes = np.arange(parity, KMAX, 2)
    mode_ids = jnp.asarray(np.concatenate([modes, modes]).astype(np.int32))
    factor = jnp.where(mode_ids == 0, jnp.float32(1.0), jnp.float32(2.0)) / NLON
    return jnp.where(mode_ids[None, :] <= cut[:, None], factor[None, :], jnp.float32(0.0))


def lowpass_rows(x, cut, tables):
    even_table, odd_table = tables
    first, second = x[:, :HALF], x[:, HALF:]
    spec_even = jnp.dot(first + second, even_table, precision=mxu_precision,
                        preferred_element_type=jnp.float32)
    spec_odd = jnp.dot(first - second, odd_table, precision=mxu_precision,
                       preferred_element_type=jnp.float32)
    dims = (((1,), (1,)), ((), ()))
    even_out = lax.dot_general(spec_even * parity_weight(0, cut), even_table, dims,
                               precision=mxu_precision, preferred_element_type=jnp.float32)
    odd_out = lax.dot_general(spec_odd * parity_weight(1, cut), odd_table, dims,
                              precision=mxu_precision, preferred_element_type=jnp.float32)
    summed = jnp.concatenate([even_out + odd_out, even_out - odd_out], axis=1)
    return jnp.where((cut < HALF)[:, None], summed, x)


def filtered(x, cut, tables):
    shape = x.shape
    rows = x.reshape(-1, NLON)
    cuts = jnp.broadcast_to(cut, shape[:-1]).reshape(-1)
    out = lax.cond(jnp.any(cut < HALF), lambda: lowpass_rows(rows, cuts, tables), lambda: rows)
    return out.reshape(shape)


def on_device(zonal_wind, merid_wind, tracer, vertical_wind, cutoff):
    lat_rows = zonal_wind.shape[1]
    lat_count = lax.axis_size("lat")
    lat_index = lax.axis_index("lat")
    total_rows = lat_rows * lat_count
    row_start = lat_index * lat_rows
    own_cut = lax.dynamic_slice_in_dim(cutoff, row_start, lat_rows)

    stacked = jnp.stack([zonal_wind, merid_wind, tracer])
    levels = stacked.shape[1]
    pole_rows = [min(j, total_rows - 1 - j) + 1 <= CAP for j in range(total_rows)]
    filter_lat = [i for i in range(lat_count) if any(pole_rows[i * lat_rows:(i + 1) * lat_rows])]
    plain_lat = [i for i in range(lat_count) if i not in filter_lat]
    top = jnp.concatenate([stacked[:, levels - 1], vertical_wind[levels - 1 :]], axis=0)
    bottom = jnp.concatenate([stacked[:, 0], vertical_wind[:1]], axis=0)
    late_lat = [i for i in range(lat_count) if i in filter_lat or i - 1 in filter_lat or i + 1 in filter_lat]
    early_lat = [i for i in range(lat_count) if i not in late_lat]
    below_plain = group_shift(top, early_lat, True)
    above_plain = group_shift(bottom, early_lat, False)

    tables = (parity_table(0), parity_table(1))
    south_plain = lat_group_shift(stacked[:, :, lat_rows - 1 :], plain_lat, True)
    north_plain = lat_group_shift(stacked[:, :, :1], plain_lat, False)
    stacked, below_plain, above_plain, south_plain, north_plain = lax.optimization_barrier(
        (stacked, below_plain, above_plain, south_plain, north_plain))
    field = filtered(stacked, own_cut, tables)
    top = jnp.concatenate([field[:, levels - 1], vertical_wind[levels - 1 :]], axis=0)
    bottom = jnp.concatenate([field[:, 0], vertical_wind[:1]], axis=0)
    below_filtered = group_shift(top, late_lat, True)
    above_filtered = group_shift(bottom, late_lat, False)
    is_late = jnp.any(lat_index == jnp.asarray(late_lat, jnp.int32))
    below_all = jnp.where(is_late, below_filtered, below_plain)
    above_all = jnp.where(is_late, above_filtered, above_plain)
    below, below_wind = below_all[:3, None], below_all[3:]
    above, above_wind = above_all[:3, None], above_all[3:]
    south_filtered = lat_group_shift(field[:, :, lat_rows - 1 :], filter_lat, True)
    north_filtered = lat_group_shift(field[:, :, :1], filter_lat, False)
    south_is_filter = jnp.any(lat_index - 1 == jnp.asarray(filter_lat, jnp.int32))
    north_is_filter = jnp.any(lat_index + 1 == jnp.asarray(filter_lat, jnp.int32))
    south = jnp.where(south_is_filter, south_filtered, south_plain)
    north = jnp.where(north_is_filter, north_filtered, north_plain)

    vertical_pad = jnp.concatenate([below_wind, vertical_wind, above_wind], axis=0)
    field_lat = jnp.concatenate([south, field, north], axis=2)
    field_lev = jnp.concatenate([below, field, above], axis=1)

    face_ids = (row_start + jnp.arange(lat_rows + 1, dtype=jnp.int32)).astype(jnp.float32)
    face_cos = jnp.sin(face_ids * (math.pi / total_rows))
    center_ids = (row_start + jnp.arange(lat_rows, dtype=jnp.int32)).astype(jnp.float32)
    center_cos = jnp.sin((center_ids + 0.5) * (math.pi / total_rows))
    zonal_now = field[0]
    east_wind = 0.5 * (zonal_now + jnp.roll(zonal_now, -1, axis=2))
    flux_x = zonal_scale * east_wind[None] * (0.5 * (field + jnp.roll(field, -1, axis=3)))
    div_x = flux_x - jnp.roll(flux_x, 1, axis=3)
    merid_lat = field_lat[1]
    north_wind = 0.5 * (merid_lat[:, :-1] + merid_lat[:, 1:])
    flux_y = (
        merid_scale
        * face_cos[None, None, :, None]
        * north_wind[None]
        * (0.5 * (field_lat[:, :, :-1] + field_lat[:, :, 1:]))
    )
    div_y = flux_y[:, :, 1:] - flux_y[:, :, :-1]
    upward = 0.5 * (vertical_pad[:-1] + vertical_pad[1:])
    flux_z = vertical_scale * upward[None] * (0.5 * (field_lev[:, :-1] + field_lev[:, 1:]))
    div_z = flux_z[:, 1:] - flux_z[:, :-1]
    updated = field - (div_x + div_y) / center_cos[None, None, :, None] - div_z
    return (updated[0], updated[1], updated[2])


def solution(mesh):
    in_specs = (
        P("lev", "lat", None),
        P("lev", "lat", None),
        P("lev", "lat", None),
        P("lev", "lat", None),
        P(),
    )
    out_specs = (P("lev", "lat", None), P("lev", "lat", None), P("lev", "lat", None))
    return jax.shard_map(
        on_device, mesh=mesh, in_specs=in_specs, out_specs=out_specs, check_vma=False
    )
```

```python
import math

import jax
import numpy as np
import jax.numpy as jnp
from jax import lax
from jax.sharding import PartitionSpec as P

NLON = 2880
KMAX = 720
HALF = NLON // 2
CAP = 80

zonal_scale = 0.1
merid_scale = 0.1
vertical_scale = 0.1
mxu_precision = lax.Precision.HIGH


def shift(x, axis, up):
    size = lax.axis_size(axis)
    pairs = [(i, i + 1) for i in range(size - 1)]
    if not up:
        pairs = [(j, i) for i, j in pairs]
    return lax.ppermute(x, axis, pairs)


def group_shift(x, lat_group, up):
    lev_size = lax.axis_size("lev")
    pairs = []
    for lat in lat_group:
        for lev in range(lev_size - 1):
            source, target = lat * lev_size + lev, lat * lev_size + lev + 1
            pairs.append((source, target) if up else (target, source))
    return lax.ppermute(x, ("lat", "lev"), pairs)


def lat_group_shift(x, sources, up):
    lat_size, lev_size = lax.axis_size("lat"), lax.axis_size("lev")
    step = 1 if up else -1
    pairs = [(lat * lev_size + lev, (lat + step) * lev_size + lev)
             for lat in sources if 0 <= lat + step < lat_size for lev in range(lev_size)]
    return lax.ppermute(x, ("lat", "lev"), pairs)


def parity_table(parity):
    low = 48
    modes = np.arange(parity, KMAX, 2)
    k = np.concatenate([modes, modes])[None, :]
    is_sin = np.arange(KMAX)[None, :] >= KMAX // 2
    step = 2.0 * np.pi / NLON
    lo = (np.arange(low)[:, None] * k) % NLON * step
    hi = (low * np.arange(HALF // low)[:, None] * k) % NLON * step
    first = np.where(is_sin, np.sin(lo), np.cos(lo))
    turn = np.where(is_sin, np.cos(lo), -np.sin(lo))
    as_f32 = lambda v: jnp.asarray(v.astype(np.float32))
    table = (as_f32(first)[None] * as_f32(np.cos(hi))[:, None]
             + as_f32(turn)[None] * as_f32(np.sin(hi))[:, None])
    return table.reshape(HALF, KMAX)


def parity_weight(parity, cut):
    modes = np.arange(parity, KMAX, 2)
    mode_ids = jnp.asarray(np.concatenate([modes, modes]).astype(np.int32))
    factor = jnp.where(mode_ids == 0, jnp.float32(1.0), jnp.float32(2.0)) / NLON
    return jnp.where(mode_ids[None, :] <= cut[:, None], factor[None, :], jnp.float32(0.0))


def lowpass_rows(x, cut, tables):
    even_table, odd_table = tables
    first, second = x[:, :HALF], x[:, HALF:]
    spec_even = jnp.dot(first + second, even_table, precision=mxu_precision,
                        preferred_element_type=jnp.float32)
    spec_odd = jnp.dot(first - second, odd_table, precision=mxu_precision,
                       preferred_element_type=jnp.float32)
    dims = (((1,), (1,)), ((), ()))
    even_out = lax.dot_general(spec_even * parity_weight(0, cut), even_table, dims,
                               precision=mxu_precision, preferred_element_type=jnp.float32)
    odd_out = lax.dot_general(spec_odd * parity_weight(1, cut), odd_table, dims,
                              precision=mxu_precision, preferred_element_type=jnp.float32)
    summed = jnp.concatenate([even_out + odd_out, even_out - odd_out], axis=1)
    return jnp.where((cut < HALF)[:, None], summed, x)


def filtered(x, cut, tables):
    shape = x.shape
    rows = x.reshape(-1, NLON)
    cuts = jnp.broadcast_to(cut, shape[:-1]).reshape(-1)
    out = lax.cond(jnp.any(cut < HALF), lambda: lowpass_rows(rows, cuts, tables), lambda: rows)
    return out.reshape(shape)


def on_device(zonal_wind, merid_wind, tracer, vertical_wind, cutoff):
    lat_rows = zonal_wind.shape[1]
    lat_count = lax.axis_size("lat")
    lat_index = lax.axis_index("lat")
    total_rows = lat_rows * lat_count
    row_start = lat_index * lat_rows
    own_cut = lax.dynamic_slice_in_dim(cutoff, row_start, lat_rows)

    stacked = jnp.stack([zonal_wind, merid_wind, tracer])
    levels = stacked.shape[1]
    pole_rows = [min(j, total_rows - 1 - j) + 1 <= CAP for j in range(total_rows)]
    filter_lat = [i for i in range(lat_count) if any(pole_rows[i * lat_rows:(i + 1) * lat_rows])]
    plain_lat = [i for i in range(lat_count) if i not in filter_lat]
    top = jnp.concatenate([stacked[:, levels - 1], vertical_wind[levels - 1 :]], axis=0)
    bottom = jnp.concatenate([stacked[:, 0], vertical_wind[:1]], axis=0)
    below_plain = group_shift(top, plain_lat, True)
    above_plain = group_shift(bottom, plain_lat, False)

    tables = (parity_table(0), parity_table(1))
    south_plain = lat_group_shift(stacked[:, :, lat_rows - 1 :], plain_lat, True)
    north_plain = lat_group_shift(stacked[:, :, :1], plain_lat, False)
    stacked, south_plain, north_plain = lax.optimization_barrier((stacked, south_plain, north_plain))
    field = filtered(stacked, own_cut, tables)
    top = jnp.concatenate([field[:, levels - 1], vertical_wind[levels - 1 :]], axis=0)
    bottom = jnp.concatenate([field[:, 0], vertical_wind[:1]], axis=0)
    below_filtered = group_shift(top, filter_lat, True)
    above_filtered = group_shift(bottom, filter_lat, False)
    is_filter = jnp.any(lat_index == jnp.asarray(filter_lat, jnp.int32))
    below_all = jnp.where(is_filter, below_filtered, below_plain)
    above_all = jnp.where(is_filter, above_filtered, above_plain)
    below, below_wind = below_all[:3, None], below_all[3:]
    above, above_wind = above_all[:3, None], above_all[3:]
    south_filtered = lat_group_shift(field[:, :, lat_rows - 1 :], filter_lat, True)
    north_filtered = lat_group_shift(field[:, :, :1], filter_lat, False)
    south_is_filter = jnp.any(lat_index - 1 == jnp.asarray(filter_lat, jnp.int32))
    north_is_filter = jnp.any(lat_index + 1 == jnp.asarray(filter_lat, jnp.int32))
    south = jnp.where(south_is_filter, south_filtered, south_plain)
    north = jnp.where(north_is_filter, north_filtered, north_plain)

    vertical_pad = jnp.concatenate([below_wind, vertical_wind, above_wind], axis=0)
    field_lat = jnp.concatenate([south, field, north], axis=2)
    field_lev = jnp.concatenate([below, field, above], axis=1)

    face_ids = (row_start + jnp.arange(lat_rows + 1, dtype=jnp.int32)).astype(jnp.float32)
    face_cos = jnp.sin(face_ids * (math.pi / total_rows))
    center_ids = (row_start + jnp.arange(lat_rows, dtype=jnp.int32)).astype(jnp.float32)
    center_cos = jnp.sin((center_ids + 0.5) * (math.pi / total_rows))
    zonal_now = field[0]
    east_wind = 0.5 * (zonal_now + jnp.roll(zonal_now, -1, axis=2))
    flux_x = zonal_scale * east_wind[None] * (0.5 * (field + jnp.roll(field, -1, axis=3)))
    div_x = flux_x - jnp.roll(flux_x, 1, axis=3)
    merid_lat = field_lat[1]
    north_wind = 0.5 * (merid_lat[:, :-1] + merid_lat[:, 1:])
    flux_y = (
        merid_scale
        * face_cos[None, None, :, None]
        * north_wind[None]
        * (0.5 * (field_lat[:, :, :-1] + field_lat[:, :, 1:]))
    )
    div_y = flux_y[:, :, 1:] - flux_y[:, :, :-1]
    upward = 0.5 * (vertical_pad[:-1] + vertical_pad[1:])
    flux_z = vertical_scale * upward[None] * (0.5 * (field_lev[:, :-1] + field_lev[:, 1:]))
    div_z = flux_z[:, 1:] - flux_z[:, :-1]
    updated = field - (div_x + div_y) / center_cos[None, None, :, None] - div_z
    return (updated[0], updated[1], updated[2])


def solution(mesh):
    in_specs = (
        P("lev", "lat", None),
        P("lev", "lat", None),
        P("lev", "lat", None),
        P("lev", "lat", None),
        P(),
    )
    out_specs = (P("lev", "lat", None), P("lev", "lat", None), P("lev", "lat", None))
    return jax.shard_map(
        on_device, mesh=mesh, in_specs=in_specs, out_specs=out_specs, check_vma=False
    )
```

```python
import math

import jax
import numpy as np
import jax.numpy as jnp
from jax import lax
from jax.sharding import PartitionSpec as P

NLON = 2880
KMAX = 720
HALF = NLON // 2
CAP = 80

zonal_scale = 0.1
merid_scale = 0.1
vertical_scale = 0.1
mxu_precision = lax.Precision.HIGH


def shift(x, axis, up):
    size = lax.axis_size(axis)
    pairs = [(i, i + 1) for i in range(size - 1)]
    if not up:
        pairs = [(j, i) for i, j in pairs]
    return lax.ppermute(x, axis, pairs)


def group_shift(x, lat_group, up):
    lev_size = lax.axis_size("lev")
    pairs = []
    for lat in lat_group:
        for lev in range(lev_size - 1):
            source, target = lat * lev_size + lev, lat * lev_size + lev + 1
            pairs.append((source, target) if up else (target, source))
    return lax.ppermute(x, ("lat", "lev"), pairs)


def lat_group_shift(x, sources, up):
    lat_size, lev_size = lax.axis_size("lat"), lax.axis_size("lev")
    step = 1 if up else -1
    pairs = [(lat * lev_size + lev, (lat + step) * lev_size + lev)
             for lat in sources if 0 <= lat + step < lat_size for lev in range(lev_size)]
    return lax.ppermute(x, ("lat", "lev"), pairs)


def parity_table(parity):
    low = 48
    modes = np.arange(parity, KMAX, 2)
    k = np.concatenate([modes, modes])[None, :]
    is_sin = np.arange(KMAX)[None, :] >= KMAX // 2
    step = 2.0 * np.pi / NLON
    lo = (np.arange(low)[:, None] * k) % NLON * step
    hi = (low * np.arange(HALF // low)[:, None] * k) % NLON * step
    first = np.where(is_sin, np.sin(lo), np.cos(lo))
    turn = np.where(is_sin, np.cos(lo), -np.sin(lo))
    as_f32 = lambda v: jnp.asarray(v.astype(np.float32))
    table = (as_f32(first)[None] * as_f32(np.cos(hi))[:, None]
             + as_f32(turn)[None] * as_f32(np.sin(hi))[:, None])
    return table.reshape(HALF, KMAX)


def parity_weight(parity, cut):
    modes = np.arange(parity, KMAX, 2)
    mode_ids = jnp.asarray(np.concatenate([modes, modes]).astype(np.int32))
    factor = jnp.where(mode_ids == 0, jnp.float32(1.0), jnp.float32(2.0)) / NLON
    return jnp.where(mode_ids[None, :] <= cut[:, None], factor[None, :], jnp.float32(0.0))


def lowpass_rows(x, cut, tables):
    even_table, odd_table = tables
    first, second = x[:, :HALF], x[:, HALF:]
    spec_even = jnp.dot(first + second, even_table, precision=mxu_precision,
                        preferred_element_type=jnp.float32)
    spec_odd = jnp.dot(first - second, odd_table, precision=mxu_precision,
                       preferred_element_type=jnp.float32)
    dims = (((1,), (1,)), ((), ()))
    even_out = lax.dot_general(spec_even * parity_weight(0, cut), even_table, dims,
                               precision=mxu_precision, preferred_element_type=jnp.float32)
    odd_out = lax.dot_general(spec_odd * parity_weight(1, cut), odd_table, dims,
                              precision=mxu_precision, preferred_element_type=jnp.float32)
    summed = jnp.concatenate([even_out + odd_out, even_out - odd_out], axis=1)
    return jnp.where((cut < HALF)[:, None], summed, x)


def filtered(x, cut, tables):
    shape = x.shape
    rows = x.reshape(-1, NLON)
    cuts = jnp.broadcast_to(cut, shape[:-1]).reshape(-1)
    out = lax.cond(jnp.any(cut < HALF), lambda: lowpass_rows(rows, cuts, tables), lambda: rows)
    return out.reshape(shape)


def on_device(zonal_wind, merid_wind, tracer, vertical_wind, cutoff):
    lat_rows = zonal_wind.shape[1]
    lat_count = lax.axis_size("lat")
    lat_index = lax.axis_index("lat")
    total_rows = lat_rows * lat_count
    row_start = lat_index * lat_rows
    own_cut = lax.dynamic_slice_in_dim(cutoff, row_start, lat_rows)

    stacked = jnp.stack([zonal_wind, merid_wind, tracer])
    levels = stacked.shape[1]
    pole_rows = [min(j, total_rows - 1 - j) + 1 <= CAP for j in range(total_rows)]
    filter_lat = [i for i in range(lat_count) if any(pole_rows[i * lat_rows:(i + 1) * lat_rows])]
    plain_lat = [i for i in range(lat_count) if i not in filter_lat]
    top = jnp.concatenate([stacked[:, levels - 1], vertical_wind[levels - 1 :]], axis=0)
    bottom = jnp.concatenate([stacked[:, 0], vertical_wind[:1]], axis=0)
    edge_lat = [i for i in plain_lat if i - 1 in filter_lat or i + 1 in filter_lat]
    inner_lat = [i for i in plain_lat if i not in edge_lat]
    below_inner = group_shift(top, inner_lat, True)
    above_inner = group_shift(bottom, inner_lat, False)
    below_edge = group_shift(top, edge_lat, True)
    above_edge = group_shift(bottom, edge_lat, False)

    tables = (parity_table(0), parity_table(1))
    south_plain = lat_group_shift(stacked[:, :, lat_rows - 1 :], plain_lat, True)
    north_plain = lat_group_shift(stacked[:, :, :1], plain_lat, False)
    stacked, below_inner, above_inner, south_plain, north_plain = lax.optimization_barrier(
        (stacked, below_inner, above_inner, south_plain, north_plain))
    is_edge = jnp.any(lat_index == jnp.asarray(edge_lat, jnp.int32))
    below_plain = jnp.where(is_edge, below_edge, below_inner)
    above_plain = jnp.where(is_edge, above_edge, above_inner)
    field = filtered(stacked, own_cut, tables)
    top = jnp.concatenate([field[:, levels - 1], vertical_wind[levels - 1 :]], axis=0)
    bottom = jnp.concatenate([field[:, 0], vertical_wind[:1]], axis=0)
    below_filtered = group_shift(top, filter_lat, True)
    above_filtered = group_shift(bottom, filter_lat, False)
    is_filter = jnp.any(lat_index == jnp.asarray(filter_lat, jnp.int32))
    below_all = jnp.where(is_filter, below_filtered, below_plain)
    above_all = jnp.where(is_filter, above_filtered, above_plain)
    below, below_wind = below_all[:3, None], below_all[3:]
    above, above_wind = above_all[:3, None], above_all[3:]
    south_filtered = lat_group_shift(field[:, :, lat_rows - 1 :], filter_lat, True)
    north_filtered = lat_group_shift(field[:, :, :1], filter_lat, False)
    south_is_filter = jnp.any(lat_index - 1 == jnp.asarray(filter_lat, jnp.int32))
    north_is_filter = jnp.any(lat_index + 1 == jnp.asarray(filter_lat, jnp.int32))
    south = jnp.where(south_is_filter, south_filtered, south_plain)
    north = jnp.where(north_is_filter, north_filtered, north_plain)

    vertical_pad = jnp.concatenate([below_wind, vertical_wind, above_wind], axis=0)
    field_lat = jnp.concatenate([south, field, north], axis=2)
    field_lev = jnp.concatenate([below, field, above], axis=1)

    face_ids = (row_start + jnp.arange(lat_rows + 1, dtype=jnp.int32)).astype(jnp.float32)
    face_cos = jnp.sin(face_ids * (math.pi / total_rows))
    center_ids = (row_start + jnp.arange(lat_rows, dtype=jnp.int32)).astype(jnp.float32)
    center_cos = jnp.sin((center_ids + 0.5) * (math.pi / total_rows))
    zonal_now = field[0]
    east_wind = 0.5 * (zonal_now + jnp.roll(zonal_now, -1, axis=2))
    flux_x = zonal_scale * east_wind[None] * (0.5 * (field + jnp.roll(field, -1, axis=3)))
    div_x = flux_x - jnp.roll(flux_x, 1, axis=3)
    merid_lat = field_lat[1]
    north_wind = 0.5 * (merid_lat[:, :-1] + merid_lat[:, 1:])
    flux_y = (
        merid_scale
        * face_cos[None, None, :, None]
        * north_wind[None]
        * (0.5 * (field_lat[:, :, :-1] + field_lat[:, :, 1:]))
    )
    div_y = flux_y[:, :, 1:] - flux_y[:, :, :-1]
    upward = 0.5 * (vertical_pad[:-1] + vertical_pad[1:])
    flux_z = vertical_scale * upward[None] * (0.5 * (field_lev[:, :-1] + field_lev[:, 1:]))
    div_z = flux_z[:, 1:] - flux_z[:, :-1]
    updated = field - (div_x + div_y) / center_cos[None, None, :, None] - div_z
    return (updated[0], updated[1], updated[2])


def solution(mesh):
    in_specs = (
        P("lev", "lat", None),
        P("lev", "lat", None),
        P("lev", "lat", None),
        P("lev", "lat", None),
        P(),
    )
    out_specs = (P("lev", "lat", None), P("lev", "lat", None), P("lev", "lat", None))
    return jax.shard_map(
        on_device, mesh=mesh, in_specs=in_specs, out_specs=out_specs, check_vma=False
    )
```

```python
import math

import jax
import numpy as np
import jax.numpy as jnp
from jax import lax
from jax.sharding import PartitionSpec as P

NLON = 2880
KMAX = 720
HALF = NLON // 2
CAP = 80

zonal_scale = 0.1
merid_scale = 0.1
vertical_scale = 0.1
mxu_precision = lax.Precision.HIGH


def shift(x, axis, up):
    size = lax.axis_size(axis)
    pairs = [(i, i + 1) for i in range(size - 1)]
    if not up:
        pairs = [(j, i) for i, j in pairs]
    return lax.ppermute(x, axis, pairs)


def group_shift(x, lat_group, up):
    lev_size = lax.axis_size("lev")
    pairs = []
    for lat in lat_group:
        for lev in range(lev_size - 1):
            source, target = lat * lev_size + lev, lat * lev_size + lev + 1
            pairs.append((source, target) if up else (target, source))
    return lax.ppermute(x, ("lat", "lev"), pairs)


def lat_group_shift(x, sources, up):
    lat_size, lev_size = lax.axis_size("lat"), lax.axis_size("lev")
    step = 1 if up else -1
    pairs = [(lat * lev_size + lev, (lat + step) * lev_size + lev)
             for lat in sources if 0 <= lat + step < lat_size for lev in range(lev_size)]
    return lax.ppermute(x, ("lat", "lev"), pairs)


def lat_pair_shift(x, sources, targets, up):
    lev_size = lax.axis_size("lev")
    step = 1 if up else -1
    pairs = [(lat * lev_size + lev, (lat + step) * lev_size + lev)
             for lat in sources if lat + step in targets for lev in range(lev_size)]
    return lax.ppermute(x, ("lat", "lev"), pairs)


def parity_table(parity):
    low = 48
    modes = np.arange(parity, KMAX, 2)
    k = np.concatenate([modes, modes])[None, :]
    is_sin = np.arange(KMAX)[None, :] >= KMAX // 2
    step = 2.0 * np.pi / NLON
    lo = (np.arange(low)[:, None] * k) % NLON * step
    hi = (low * np.arange(HALF // low)[:, None] * k) % NLON * step
    first = np.where(is_sin, np.sin(lo), np.cos(lo))
    turn = np.where(is_sin, np.cos(lo), -np.sin(lo))
    as_f32 = lambda v: jnp.asarray(v.astype(np.float32))
    table = (as_f32(first)[None] * as_f32(np.cos(hi))[:, None]
             + as_f32(turn)[None] * as_f32(np.sin(hi))[:, None])
    return table.reshape(HALF, KMAX)


def parity_weight(parity, cut):
    modes = np.arange(parity, KMAX, 2)
    mode_ids = jnp.asarray(np.concatenate([modes, modes]).astype(np.int32))
    factor = jnp.where(mode_ids == 0, jnp.float32(1.0), jnp.float32(2.0)) / NLON
    return jnp.where(mode_ids[None, :] <= cut[:, None], factor[None, :], jnp.float32(0.0))


def lowpass_rows(x, cut, tables):
    even_table, odd_table = tables
    first, second = x[:, :HALF], x[:, HALF:]
    spec_even = jnp.dot(first + second, even_table, precision=mxu_precision,
                        preferred_element_type=jnp.float32)
    spec_odd = jnp.dot(first - second, odd_table, precision=mxu_precision,
                       preferred_element_type=jnp.float32)
    dims = (((1,), (1,)), ((), ()))
    even_out = lax.dot_general(spec_even * parity_weight(0, cut), even_table, dims,
                               precision=mxu_precision, preferred_element_type=jnp.float32)
    odd_out = lax.dot_general(spec_odd * parity_weight(1, cut), odd_table, dims,
                              precision=mxu_precision, preferred_element_type=jnp.float32)
    summed = jnp.concatenate([even_out + odd_out, even_out - odd_out], axis=1)
    return jnp.where((cut < HALF)[:, None], summed, x)


def filtered(x, cut, tables):
    shape = x.shape
    rows = x.reshape(-1, NLON)
    cuts = jnp.broadcast_to(cut, shape[:-1]).reshape(-1)
    out = lax.cond(jnp.any(cut < HALF), lambda: lowpass_rows(rows, cuts, tables), lambda: rows)
    return out.reshape(shape)


def on_device(zonal_wind, merid_wind, tracer, vertical_wind, cutoff):
    lat_rows = zonal_wind.shape[1]
    lat_count = lax.axis_size("lat")
    lat_index = lax.axis_index("lat")
    total_rows = lat_rows * lat_count
    row_start = lat_index * lat_rows
    own_cut = lax.dynamic_slice_in_dim(cutoff, row_start, lat_rows)

    stacked = jnp.stack([zonal_wind, merid_wind, tracer])
    levels = stacked.shape[1]
    pole_rows = [min(j, total_rows - 1 - j) + 1 <= CAP for j in range(total_rows)]
    filter_lat = [i for i in range(lat_count) if any(pole_rows[i * lat_rows:(i + 1) * lat_rows])]
    plain_lat = [i for i in range(lat_count) if i not in filter_lat]
    top = jnp.concatenate([stacked[:, levels - 1], vertical_wind[levels - 1 :]], axis=0)
    bottom = jnp.concatenate([stacked[:, 0], vertical_wind[:1]], axis=0)
    below_plain = group_shift(top, plain_lat, True)
    above_plain = group_shift(bottom, plain_lat, False)

    tables = (parity_table(0), parity_table(1))
    south_plain = lat_group_shift(stacked[:, :, lat_rows - 1 :], plain_lat, True)
    north_plain = lat_group_shift(stacked[:, :, :1], plain_lat, False)
    stacked, below_plain, above_plain, south_plain, north_plain = lax.optimization_barrier(
        (stacked, below_plain, above_plain, south_plain, north_plain))
    field = filtered(stacked, own_cut, tables)
    top = jnp.concatenate([field[:, levels - 1], vertical_wind[levels - 1 :]], axis=0)
    bottom = jnp.concatenate([field[:, 0], vertical_wind[:1]], axis=0)
    below_filtered = group_shift(top, filter_lat, True)
    above_filtered = group_shift(bottom, filter_lat, False)
    is_filter = jnp.any(lat_index == jnp.asarray(filter_lat, jnp.int32))
    below_all = jnp.where(is_filter, below_filtered, below_plain)
    above_all = jnp.where(is_filter, above_filtered, above_plain)
    below, below_wind = below_all[:3, None], below_all[3:]
    above, above_wind = above_all[:3, None], above_all[3:]
    south_inner = lat_pair_shift(field[:, :, lat_rows - 1 :], filter_lat, filter_lat, True)
    north_inner = lat_pair_shift(field[:, :, :1], filter_lat, filter_lat, False)
    south_source, north_source, _ = lax.optimization_barrier(
        (field[:, :, lat_rows - 1 :], field[:, :, :1], (below_filtered, above_filtered)))
    south_edge = lat_pair_shift(south_source, filter_lat, plain_lat, True)
    north_edge = lat_pair_shift(north_source, filter_lat, plain_lat, False)
    south_filtered = jnp.where(is_filter, south_inner, south_edge)
    north_filtered = jnp.where(is_filter, north_inner, north_edge)
    south_is_filter = jnp.any(lat_index - 1 == jnp.asarray(filter_lat, jnp.int32))
    north_is_filter = jnp.any(lat_index + 1 == jnp.asarray(filter_lat, jnp.int32))
    south = jnp.where(south_is_filter, south_filtered, south_plain)
    north = jnp.where(north_is_filter, north_filtered, north_plain)

    vertical_pad = jnp.concatenate([below_wind, vertical_wind, above_wind], axis=0)
    field_lat = jnp.concatenate([south, field, north], axis=2)
    field_lev = jnp.concatenate([below, field, above], axis=1)

    face_ids = (row_start + jnp.arange(lat_rows + 1, dtype=jnp.int32)).astype(jnp.float32)
    face_cos = jnp.sin(face_ids * (math.pi / total_rows))
    center_ids = (row_start + jnp.arange(lat_rows, dtype=jnp.int32)).astype(jnp.float32)
    center_cos = jnp.sin((center_ids + 0.5) * (math.pi / total_rows))
    zonal_now = field[0]
    east_wind = 0.5 * (zonal_now + jnp.roll(zonal_now, -1, axis=2))
    flux_x = zonal_scale * east_wind[None] * (0.5 * (field + jnp.roll(field, -1, axis=3)))
    div_x = flux_x - jnp.roll(flux_x, 1, axis=3)
    merid_lat = field_lat[1]
    north_wind = 0.5 * (merid_lat[:, :-1] + merid_lat[:, 1:])
    flux_y = (
        merid_scale
        * face_cos[None, None, :, None]
        * north_wind[None]
        * (0.5 * (field_lat[:, :, :-1] + field_lat[:, :, 1:]))
    )
    div_y = flux_y[:, :, 1:] - flux_y[:, :, :-1]
    upward = 0.5 * (vertical_pad[:-1] + vertical_pad[1:])
    flux_z = vertical_scale * upward[None] * (0.5 * (field_lev[:, :-1] + field_lev[:, 1:]))
    div_z = flux_z[:, 1:] - flux_z[:, :-1]
    updated = field - (div_x + div_y) / center_cos[None, None, :, None] - div_z
    return (updated[0], updated[1], updated[2])


def solution(mesh):
    in_specs = (
        P("lev", "lat", None),
        P("lev", "lat", None),
        P("lev", "lat", None),
        P("lev", "lat", None),
        P(),
    )
    out_specs = (P("lev", "lat", None), P("lev", "lat", None), P("lev", "lat", None))
    return jax.shard_map(
        on_device, mesh=mesh, in_specs=in_specs, out_specs=out_specs, check_vma=False
    )
```

```python
import math

import jax
import numpy as np
import jax.numpy as jnp
from jax import lax
from jax.sharding import PartitionSpec as P

NLON = 2880
KMAX = 720
HALF = NLON // 2
CAP = 80

zonal_scale = 0.1
merid_scale = 0.1
vertical_scale = 0.1
mxu_precision = lax.Precision.HIGH


def shift(x, axis, up):
    size = lax.axis_size(axis)
    pairs = [(i, i + 1) for i in range(size - 1)]
    if not up:
        pairs = [(j, i) for i, j in pairs]
    return lax.ppermute(x, axis, pairs)


def group_shift(x, lat_group, up):
    lev_size = lax.axis_size("lev")
    pairs = []
    for lat in lat_group:
        for lev in range(lev_size - 1):
            source, target = lat * lev_size + lev, lat * lev_size + lev + 1
            pairs.append((source, target) if up else (target, source))
    return lax.ppermute(x, ("lat", "lev"), pairs)


def lat_group_shift(x, sources, up):
    lat_size, lev_size = lax.axis_size("lat"), lax.axis_size("lev")
    step = 1 if up else -1
    pairs = [(lat * lev_size + lev, (lat + step) * lev_size + lev)
             for lat in sources if 0 <= lat + step < lat_size for lev in range(lev_size)]
    return lax.ppermute(x, ("lat", "lev"), pairs)


def parity_table(parity):
    low = 48
    modes = np.arange(parity, KMAX, 2)
    k = np.concatenate([modes, modes])[None, :]
    is_sin = np.arange(KMAX)[None, :] >= KMAX // 2
    step = 2.0 * np.pi / NLON
    lo = (np.arange(low)[:, None] * k) % NLON * step
    hi = (low * np.arange(HALF // low)[:, None] * k) % NLON * step
    first = np.where(is_sin, np.sin(lo), np.cos(lo))
    turn = np.where(is_sin, np.cos(lo), -np.sin(lo))
    as_f32 = lambda v: jnp.asarray(v.astype(np.float32))
    table = (as_f32(first)[None] * as_f32(np.cos(hi))[:, None]
             + as_f32(turn)[None] * as_f32(np.sin(hi))[:, None])
    return table.reshape(HALF, KMAX)


def parity_weight(parity, cut):
    modes = np.arange(parity, KMAX, 2)
    mode_ids = jnp.asarray(np.concatenate([modes, modes]).astype(np.int32))
    factor = jnp.where(mode_ids == 0, jnp.float32(1.0), jnp.float32(2.0)) / NLON
    return jnp.where(mode_ids[None, :] <= cut[:, None], factor[None, :], jnp.float32(0.0))


def lowpass_rows(x, cut, tables):
    even_table, odd_table = tables
    first, second = x[:, :HALF], x[:, HALF:]
    spec_even = jnp.dot(first + second, even_table, precision=mxu_precision,
                        preferred_element_type=jnp.float32)
    spec_odd = jnp.dot(first - second, odd_table, precision=mxu_precision,
                       preferred_element_type=jnp.float32)
    dims = (((1,), (1,)), ((), ()))
    even_out = lax.dot_general(spec_even * parity_weight(0, cut), even_table, dims,
                               precision=mxu_precision, preferred_element_type=jnp.float32)
    odd_out = lax.dot_general(spec_odd * parity_weight(1, cut), odd_table, dims,
                              precision=mxu_precision, preferred_element_type=jnp.float32)
    summed = jnp.concatenate([even_out + odd_out, even_out - odd_out], axis=1)
    return jnp.where((cut < HALF)[:, None], summed, x)


def filtered(x, cut, tables):
    shape = x.shape
    rows = x.reshape(-1, NLON)
    cuts = jnp.broadcast_to(cut, shape[:-1]).reshape(-1)
    out = lax.cond(jnp.any(cut < HALF), lambda: lowpass_rows(rows, cuts, tables), lambda: rows)
    return out.reshape(shape)


def on_device(zonal_wind, merid_wind, tracer, vertical_wind, cutoff):
    lat_rows = zonal_wind.shape[1]
    lat_count = lax.axis_size("lat")
    lat_index = lax.axis_index("lat")
    total_rows = lat_rows * lat_count
    row_start = lat_index * lat_rows
    own_cut = lax.dynamic_slice_in_dim(cutoff, row_start, lat_rows)

    stacked = jnp.stack([zonal_wind, merid_wind, tracer])
    levels = stacked.shape[1]
    pole_rows = [min(j, total_rows - 1 - j) + 1 <= CAP for j in range(total_rows)]
    filter_lat = [i for i in range(lat_count) if any(pole_rows[i * lat_rows:(i + 1) * lat_rows])]
    plain_lat = [i for i in range(lat_count) if i not in filter_lat]
    top = jnp.concatenate([stacked[:, levels - 1], vertical_wind[levels - 1 :]], axis=0)
    bottom = jnp.concatenate([stacked[:, 0], vertical_wind[:1]], axis=0)
    below_plain = group_shift(top, plain_lat, True)
    above_plain = group_shift(bottom, plain_lat, False)

    below_wind_f = group_shift(vertical_wind[levels - 1 :], filter_lat, True)
    above_wind_f = group_shift(vertical_wind[:1], filter_lat, False)
    tables = (parity_table(0), parity_table(1))
    south_plain = lat_group_shift(stacked[:, :, lat_rows - 1 :], plain_lat, True)
    north_plain = lat_group_shift(stacked[:, :, :1], plain_lat, False)
    stacked, below_plain, above_plain, south_plain, north_plain = lax.optimization_barrier(
        (stacked, below_plain, above_plain, south_plain, north_plain))
    field = filtered(stacked, own_cut, tables)
    below_filtered = group_shift(field[:, levels - 1], filter_lat, True)
    above_filtered = group_shift(field[:, 0], filter_lat, False)
    is_filter = jnp.any(lat_index == jnp.asarray(filter_lat, jnp.int32))
    below = jnp.where(is_filter, below_filtered, below_plain[:3])[:, None]
    above = jnp.where(is_filter, above_filtered, above_plain[:3])[:, None]
    below_wind = jnp.where(is_filter, below_wind_f, below_plain[3:])
    above_wind = jnp.where(is_filter, above_wind_f, above_plain[3:])
    south_filtered = lat_group_shift(field[:, :, lat_rows - 1 :], filter_lat, True)
    north_filtered = lat_group_shift(field[:, :, :1], filter_lat, False)
    south_is_filter = jnp.any(lat_index - 1 == jnp.asarray(filter_lat, jnp.int32))
    north_is_filter = jnp.any(lat_index + 1 == jnp.asarray(filter_lat, jnp.int32))
    south = jnp.where(south_is_filter, south_filtered, south_plain)
    north = jnp.where(north_is_filter, north_filtered, north_plain)

    vertical_pad = jnp.concatenate([below_wind, vertical_wind, above_wind], axis=0)
    field_lat = jnp.concatenate([south, field, north], axis=2)
    field_lev = jnp.concatenate([below, field, above], axis=1)

    face_ids = (row_start + jnp.arange(lat_rows + 1, dtype=jnp.int32)).astype(jnp.float32)
    face_cos = jnp.sin(face_ids * (math.pi / total_rows))
    center_ids = (row_start + jnp.arange(lat_rows, dtype=jnp.int32)).astype(jnp.float32)
    center_cos = jnp.sin((center_ids + 0.5) * (math.pi / total_rows))
    zonal_now = field[0]
    east_wind = 0.5 * (zonal_now + jnp.roll(zonal_now, -1, axis=2))
    flux_x = zonal_scale * east_wind[None] * (0.5 * (field + jnp.roll(field, -1, axis=3)))
    div_x = flux_x - jnp.roll(flux_x, 1, axis=3)
    merid_lat = field_lat[1]
    north_wind = 0.5 * (merid_lat[:, :-1] + merid_lat[:, 1:])
    flux_y = (
        merid_scale
        * face_cos[None, None, :, None]
        * north_wind[None]
        * (0.5 * (field_lat[:, :, :-1] + field_lat[:, :, 1:]))
    )
    div_y = flux_y[:, :, 1:] - flux_y[:, :, :-1]
    upward = 0.5 * (vertical_pad[:-1] + vertical_pad[1:])
    flux_z = vertical_scale * upward[None] * (0.5 * (field_lev[:, :-1] + field_lev[:, 1:]))
    div_z = flux_z[:, 1:] - flux_z[:, :-1]
    updated = field - (div_x + div_y) / center_cos[None, None, :, None] - div_z
    return (updated[0], updated[1], updated[2])


def solution(mesh):
    in_specs = (
        P("lev", "lat", None),
        P("lev", "lat", None),
        P("lev", "lat", None),
        P("lev", "lat", None),
        P(),
    )
    out_specs = (P("lev", "lat", None), P("lev", "lat", None), P("lev", "lat", None))
    return jax.shard_map(
        on_device, mesh=mesh, in_specs=in_specs, out_specs=out_specs, check_vma=False
    )
```

```python
import math

import jax
import numpy as np
import jax.numpy as jnp
from jax import lax
from jax.sharding import PartitionSpec as P

NLON = 2880
KMAX = 720
HALF = NLON // 2
CAP = 80

zonal_scale = 0.1
merid_scale = 0.1
vertical_scale = 0.1
mxu_precision = lax.Precision.HIGH


def shift(x, axis, up):
    size = lax.axis_size(axis)
    pairs = [(i, i + 1) for i in range(size - 1)]
    if not up:
        pairs = [(j, i) for i, j in pairs]
    return lax.ppermute(x, axis, pairs)


def group_shift(x, lat_group, up):
    lev_size = lax.axis_size("lev")
    pairs = []
    for lat in lat_group:
        for lev in range(lev_size - 1):
            source, target = lat * lev_size + lev, lat * lev_size + lev + 1
            pairs.append((source, target) if up else (target, source))
    return lax.ppermute(x, ("lat", "lev"), pairs)


def lat_group_shift(x, sources, up):
    lat_size, lev_size = lax.axis_size("lat"), lax.axis_size("lev")
    step = 1 if up else -1
    pairs = [(lat * lev_size + lev, (lat + step) * lev_size + lev)
             for lat in sources if 0 <= lat + step < lat_size for lev in range(lev_size)]
    return lax.ppermute(x, ("lat", "lev"), pairs)


def parity_table(parity):
    low = 48
    modes = np.arange(parity, KMAX, 2)
    k = np.concatenate([modes, modes])[None, :]
    is_sin = np.arange(KMAX)[None, :] >= KMAX // 2
    step = 2.0 * np.pi / NLON
    lo = (np.arange(low)[:, None] * k) % NLON * step
    hi = (low * np.arange(HALF // low)[:, None] * k) % NLON * step
    first = np.where(is_sin, np.sin(lo), np.cos(lo))
    turn = np.where(is_sin, np.cos(lo), -np.sin(lo))
    as_f32 = lambda v: jnp.asarray(v.astype(np.float32))
    table = (as_f32(first)[None] * as_f32(np.cos(hi))[:, None]
             + as_f32(turn)[None] * as_f32(np.sin(hi))[:, None])
    return table.reshape(HALF, KMAX)


def parity_weight(parity, cut):
    modes = np.arange(parity, KMAX, 2)
    mode_ids = jnp.asarray(np.concatenate([modes, modes]).astype(np.int32))
    factor = jnp.where(mode_ids == 0, jnp.float32(1.0), jnp.float32(2.0)) / NLON
    return jnp.where(mode_ids[None, :] <= cut[:, None], factor[None, :], jnp.float32(0.0))


def lowpass_rows(x, cut, tables):
    even_table, odd_table = tables
    first, second = x[:, :HALF], x[:, HALF:]
    spec_even = jnp.dot(first + second, even_table, precision=mxu_precision,
                        preferred_element_type=jnp.float32)
    spec_odd = jnp.dot(first - second, odd_table, precision=mxu_precision,
                       preferred_element_type=jnp.float32)
    dims = (((1,), (1,)), ((), ()))
    even_out = lax.dot_general(spec_even * parity_weight(0, cut), even_table, dims,
                               precision=mxu_precision, preferred_element_type=jnp.float32)
    odd_out = lax.dot_general(spec_odd * parity_weight(1, cut), odd_table, dims,
                              precision=mxu_precision, preferred_element_type=jnp.float32)
    summed = jnp.concatenate([even_out + odd_out, even_out - odd_out], axis=1)
    return jnp.where((cut < HALF)[:, None], summed, x)


def filtered(x, cut, tables):
    shape = x.shape
    rows = x.reshape(-1, NLON)
    cuts = jnp.broadcast_to(cut, shape[:-1]).reshape(-1)
    out = lax.cond(jnp.any(cut < HALF), lambda: lowpass_rows(rows, cuts, tables), lambda: rows)
    return out.reshape(shape)


def on_device(zonal_wind, merid_wind, tracer, vertical_wind, cutoff):
    lat_rows = zonal_wind.shape[1]
    lat_count = lax.axis_size("lat")
    lat_index = lax.axis_index("lat")
    total_rows = lat_rows * lat_count
    row_start = lat_index * lat_rows
    own_cut = lax.dynamic_slice_in_dim(cutoff, row_start, lat_rows)

    stacked = jnp.stack([zonal_wind, merid_wind, tracer])
    levels = stacked.shape[1]
    pole_rows = [min(j, total_rows - 1 - j) + 1 <= CAP for j in range(total_rows)]
    filter_lat = [i for i in range(lat_count) if any(pole_rows[i * lat_rows:(i + 1) * lat_rows])]
    plain_lat = [i for i in range(lat_count) if i not in filter_lat]
    top = jnp.concatenate([stacked[:, levels - 1], vertical_wind[levels - 1 :]], axis=0)
    bottom = jnp.concatenate([stacked[:, 0], vertical_wind[:1]], axis=0)
    below_plain = group_shift(top, plain_lat, True)
    above_plain = group_shift(bottom, plain_lat, False)

    tables = (parity_table(0), parity_table(1))
    south_plain = lat_group_shift(stacked[:, :, lat_rows - 1 :], plain_lat, True)
    north_plain = lat_group_shift(stacked[:, :, :1], plain_lat, False)
    stacked, below_plain, above_plain = lax.optimization_barrier((stacked, below_plain, above_plain))
    field = filtered(stacked, own_cut, tables)
    top = jnp.concatenate([field[:, levels - 1], vertical_wind[levels - 1 :]], axis=0)
    bottom = jnp.concatenate([field[:, 0], vertical_wind[:1]], axis=0)
    below_filtered = group_shift(top, filter_lat, True)
    above_filtered = group_shift(bottom, filter_lat, False)
    is_filter = jnp.any(lat_index == jnp.asarray(filter_lat, jnp.int32))
    below_all = jnp.where(is_filter, below_filtered, below_plain)
    above_all = jnp.where(is_filter, above_filtered, above_plain)
    below, below_wind = below_all[:3, None], below_all[3:]
    above, above_wind = above_all[:3, None], above_all[3:]
    south_filtered = lat_group_shift(field[:, :, lat_rows - 1 :], filter_lat, True)
    north_filtered = lat_group_shift(field[:, :, :1], filter_lat, False)
    south_is_filter = jnp.any(lat_index - 1 == jnp.asarray(filter_lat, jnp.int32))
    north_is_filter = jnp.any(lat_index + 1 == jnp.asarray(filter_lat, jnp.int32))
    south = jnp.where(south_is_filter, south_filtered, south_plain)
    north = jnp.where(north_is_filter, north_filtered, north_plain)

    vertical_pad = jnp.concatenate([below_wind, vertical_wind, above_wind], axis=0)
    field_lat = jnp.concatenate([south, field, north], axis=2)
    field_lev = jnp.concatenate([below, field, above], axis=1)

    face_ids = (row_start + jnp.arange(lat_rows + 1, dtype=jnp.int32)).astype(jnp.float32)
    face_cos = jnp.sin(face_ids * (math.pi / total_rows))
    center_ids = (row_start + jnp.arange(lat_rows, dtype=jnp.int32)).astype(jnp.float32)
    center_cos = jnp.sin((center_ids + 0.5) * (math.pi / total_rows))
    zonal_now = field[0]
    east_wind = 0.5 * (zonal_now + jnp.roll(zonal_now, -1, axis=2))
    flux_x = zonal_scale * east_wind[None] * (0.5 * (field + jnp.roll(field, -1, axis=3)))
    div_x = flux_x - jnp.roll(flux_x, 1, axis=3)
    merid_lat = field_lat[1]
    north_wind = 0.5 * (merid_lat[:, :-1] + merid_lat[:, 1:])
    flux_y = (
        merid_scale
        * face_cos[None, None, :, None]
        * north_wind[None]
        * (0.5 * (field_lat[:, :, :-1] + field_lat[:, :, 1:]))
    )
    div_y = flux_y[:, :, 1:] - flux_y[:, :, :-1]
    upward = 0.5 * (vertical_pad[:-1] + vertical_pad[1:])
    flux_z = vertical_scale * upward[None] * (0.5 * (field_lev[:, :-1] + field_lev[:, 1:]))
    div_z = flux_z[:, 1:] - flux_z[:, :-1]
    updated = field - (div_x + div_y) / center_cos[None, None, :, None] - div_z
    return (updated[0], updated[1], updated[2])


def solution(mesh):
    in_specs = (
        P("lev", "lat", None),
        P("lev", "lat", None),
        P("lev", "lat", None),
        P("lev", "lat", None),
        P(),
    )
    out_specs = (P("lev", "lat", None), P("lev", "lat", None), P("lev", "lat", None))
    return jax.shard_map(
        on_device, mesh=mesh, in_specs=in_specs, out_specs=out_specs, check_vma=False
    )
```

```python
import math

import jax
import numpy as np
import jax.numpy as jnp
from jax import lax
from jax.sharding import PartitionSpec as P

NLON = 2880
KMAX = 720
HALF = NLON // 2
CAP = 80

zonal_scale = 0.1
merid_scale = 0.1
vertical_scale = 0.1
mxu_precision = lax.Precision.HIGH


def shift(x, axis, up):
    size = lax.axis_size(axis)
    pairs = [(i, i + 1) for i in range(size - 1)]
    if not up:
        pairs = [(j, i) for i, j in pairs]
    return lax.ppermute(x, axis, pairs)


def group_shift(x, lat_group, up):
    lev_size = lax.axis_size("lev")
    pairs = []
    for lat in lat_group:
        for lev in range(lev_size - 1):
            source, target = lat * lev_size + lev, lat * lev_size + lev + 1
            pairs.append((source, target) if up else (target, source))
    return lax.ppermute(x, ("lat", "lev"), pairs)


def lat_group_shift(x, sources, up):
    lat_size, lev_size = lax.axis_size("lat"), lax.axis_size("lev")
    step = 1 if up else -1
    pairs = [(lat * lev_size + lev, (lat + step) * lev_size + lev)
             for lat in sources if 0 <= lat + step < lat_size for lev in range(lev_size)]
    return lax.ppermute(x, ("lat", "lev"), pairs)


def parity_table(parity):
    low = 48
    modes = np.arange(parity, KMAX, 2)
    k = np.concatenate([modes, modes])[None, :]
    is_sin = np.arange(KMAX)[None, :] >= KMAX // 2
    step = 2.0 * np.pi / NLON
    lo = (np.arange(low)[:, None] * k) % NLON * step
    hi = (low * np.arange(HALF // low)[:, None] * k) % NLON * step
    first = np.where(is_sin, np.sin(lo), np.cos(lo))
    turn = np.where(is_sin, np.cos(lo), -np.sin(lo))
    as_f32 = lambda v: jnp.asarray(v.astype(np.float32))
    table = (as_f32(first)[None] * as_f32(np.cos(hi))[:, None]
             + as_f32(turn)[None] * as_f32(np.sin(hi))[:, None])
    return table.reshape(HALF, KMAX)


def parity_weight(parity, cut):
    modes = np.arange(parity, KMAX, 2)
    mode_ids = jnp.asarray(np.concatenate([modes, modes]).astype(np.int32))
    factor = jnp.where(mode_ids == 0, jnp.float32(1.0), jnp.float32(2.0)) / NLON
    return jnp.where(mode_ids[None, :] <= cut[:, None], factor[None, :], jnp.float32(0.0))


def lowpass_rows(x, cut, tables):
    even_table, odd_table = tables
    first, second = x[:, :HALF], x[:, HALF:]
    spec_even = jnp.dot(first + second, even_table, precision=mxu_precision,
                        preferred_element_type=jnp.float32)
    spec_odd = jnp.dot(first - second, odd_table, precision=mxu_precision,
                       preferred_element_type=jnp.float32)
    dims = (((1,), (1,)), ((), ()))
    even_out = lax.dot_general(spec_even * parity_weight(0, cut), even_table, dims,
                               precision=mxu_precision, preferred_element_type=jnp.float32)
    odd_out = lax.dot_general(spec_odd * parity_weight(1, cut), odd_table, dims,
                              precision=mxu_precision, preferred_element_type=jnp.float32)
    summed = jnp.concatenate([even_out + odd_out, even_out - odd_out], axis=1)
    return jnp.where((cut < HALF)[:, None], summed, x)


def filtered(x, cut, tables):
    shape = x.shape
    rows = x.reshape(-1, NLON)
    cuts = jnp.broadcast_to(cut, shape[:-1]).reshape(-1)
    out = lax.cond(jnp.any(cut < HALF), lambda: lowpass_rows(rows, cuts, tables), lambda: rows)
    return out.reshape(shape)


def on_device(zonal_wind, merid_wind, tracer, vertical_wind, cutoff):
    lat_rows = zonal_wind.shape[1]
    lat_count = lax.axis_size("lat")
    lat_index = lax.axis_index("lat")
    total_rows = lat_rows * lat_count
    row_start = lat_index * lat_rows
    own_cut = lax.dynamic_slice_in_dim(cutoff, row_start, lat_rows)

    stacked = jnp.stack([zonal_wind, merid_wind, tracer])
    levels = stacked.shape[1]
    pole_rows = [min(j, total_rows - 1 - j) + 1 <= CAP for j in range(total_rows)]
    filter_lat = [i for i in range(lat_count) if any(pole_rows[i * lat_rows:(i + 1) * lat_rows])]
    plain_lat = [i for i in range(lat_count) if i not in filter_lat]
    top = jnp.concatenate([stacked[:, levels - 1], vertical_wind[levels - 1 :]], axis=0)
    bottom = jnp.concatenate([stacked[:, 0], vertical_wind[:1]], axis=0)
    below_plain = group_shift(top, plain_lat, True)
    above_plain = group_shift(bottom, plain_lat, False)

    tables = (parity_table(0), parity_table(1))
    south_plain = lat_group_shift(stacked[:, :, lat_rows - 1 :], plain_lat, True)
    north_plain = lat_group_shift(stacked[:, :, :1], plain_lat, False)
    stacked, below_plain, above_plain = lax.optimization_barrier((stacked, below_plain, above_plain))
    field = filtered(stacked, own_cut, tables)
    top = jnp.concatenate([field[:, levels - 1], vertical_wind[levels - 1 :]], axis=0)
    bottom = jnp.concatenate([field[:, 0], vertical_wind[:1]], axis=0)
    below_filtered = group_shift(top, filter_lat, True)
    above_filtered = group_shift(bottom, filter_lat, False)
    is_filter = jnp.any(lat_index == jnp.asarray(filter_lat, jnp.int32))
    below_all = jnp.where(is_filter, below_filtered, below_plain)
    above_all = jnp.where(is_filter, above_filtered, above_plain)
    below, below_wind = below_all[:3, None], below_all[3:]
    above, above_wind = above_all[:3, None], above_all[3:]
    south_source, north_source, _ = lax.optimization_barrier(
        (field[:, :, lat_rows - 1 :], field[:, :, :1], (below_filtered, above_filtered)))
    south_filtered = lat_group_shift(south_source, filter_lat, True)
    north_filtered = lat_group_shift(north_source, filter_lat, False)
    south_is_filter = jnp.any(lat_index - 1 == jnp.asarray(filter_lat, jnp.int32))
    north_is_filter = jnp.any(lat_index + 1 == jnp.asarray(filter_lat, jnp.int32))
    south = jnp.where(south_is_filter, south_filtered, south_plain)
    north = jnp.where(north_is_filter, north_filtered, north_plain)

    vertical_pad = jnp.concatenate([below_wind, vertical_wind, above_wind], axis=0)
    field_lat = jnp.concatenate([south, field, north], axis=2)
    field_lev = jnp.concatenate([below, field, above], axis=1)

    face_ids = (row_start + jnp.arange(lat_rows + 1, dtype=jnp.int32)).astype(jnp.float32)
    face_cos = jnp.sin(face_ids * (math.pi / total_rows))
    center_ids = (row_start + jnp.arange(lat_rows, dtype=jnp.int32)).astype(jnp.float32)
    center_cos = jnp.sin((center_ids + 0.5) * (math.pi / total_rows))
    zonal_now = field[0]
    east_wind = 0.5 * (zonal_now + jnp.roll(zonal_now, -1, axis=2))
    flux_x = zonal_scale * east_wind[None] * (0.5 * (field + jnp.roll(field, -1, axis=3)))
    div_x = flux_x - jnp.roll(flux_x, 1, axis=3)
    merid_lat = field_lat[1]
    north_wind = 0.5 * (merid_lat[:, :-1] + merid_lat[:, 1:])
    flux_y = (
        merid_scale
        * face_cos[None, None, :, None]
        * north_wind[None]
        * (0.5 * (field_lat[:, :, :-1] + field_lat[:, :, 1:]))
    )
    div_y = flux_y[:, :, 1:] - flux_y[:, :, :-1]
    upward = 0.5 * (vertical_pad[:-1] + vertical_pad[1:])
    flux_z = vertical_scale * upward[None] * (0.5 * (field_lev[:, :-1] + field_lev[:, 1:]))
    div_z = flux_z[:, 1:] - flux_z[:, :-1]
    updated = field - (div_x + div_y) / center_cos[None, None, :, None] - div_z
    return (updated[0], updated[1], updated[2])


def solution(mesh):
    in_specs = (
        P("lev", "lat", None),
        P("lev", "lat", None),
        P("lev", "lat", None),
        P("lev", "lat", None),
        P(),
    )
    out_specs = (P("lev", "lat", None), P("lev", "lat", None), P("lev", "lat", None))
    return jax.shard_map(
        on_device, mesh=mesh, in_specs=in_specs, out_specs=out_specs, check_vma=False
    )
```
